512 devices in a mesh: pb: 32 (over y, x), ka: 16 (over z, core).
Axes of the slice: x: 4, y: 8, z: 8, core: 2. Of those that a mesh axis runs over, the one named last changes fastest.
Arguments:
- queries: bfloat16 [65536, 1536], P(('pb', 'ka')), may hold values from -6 to 6
- keys: bfloat16 [65536, 1536], P(('pb', 'ka')), may hold values from -6 to 6
- values: bfloat16 [65536, 1536], P(('pb', 'ka')), may hold values from -6 to 6
- adjacency: int32 [512, 24], P(('pb', 'ka')), may hold values from -1 to 511, as said below
- counts: int32 [512], P(('pb', 'ka')), may hold values from 1 to 24, as said below
Outputs:
- attended: bfloat16 [65536, 1536], P(('pb', 'ka'))
The draws below stay inside these ranges and needn't reach their ends.
Inputs may be any that keep to these rules, and one draw needn't show every extreme that they name: adjacency[i, 0] = i; entries 1 to counts[i] - 1 are distinct blocks from i - 31 to i - 1; the other entries are -1. counts[i] is at most min(i + 1, 32); the last block lists exactly 24.
All inputs are finite; a program needn't handle non-finite values.
Results may differ from the reference program's by a relative error of at most 0.0053.
Values may be sent and summed in bfloat16 or wider, within the bound.
No kernel may reach another device: no remote copies, remote signals or barrier semaphores. Data moves between devices by JAX's collectives and lax.ppermute only.
A program may use at most 128 MiB of HBM per device.

```python
import math
import jax
import jax.numpy as jnp
from jax import lax

H = 12
DH = 128
BLK = 128
NB = 512
TOKENS = 65536
WIN = 32
KMAX = 24
N_KA = 16


def draw_queries(key, part):
    entries = jnp.clip(jax.random.normal(jax.random.fold_in(key, 3), (TOKENS, H * DH)), -6.0, 6.0)
    return entries.astype(jnp.bfloat16)


def draw_keys(key, part):
    entries = jnp.clip(jax.random.normal(jax.random.fold_in(key, 5), (TOKENS, H * DH)), -6.0, 6.0)
    return entries.astype(jnp.bfloat16)


def relation(key):
    seeded = jax.random.fold_in(key, 7)
    first_key, second_key = jax.random.split(seeded)
    block_col = jnp.arange(NB, dtype=jnp.int32)[:, None]
    offsets = jnp.arange(1, WIN, dtype=jnp.int32)[None, :]
    ranking = jax.random.randint(first_key, (NB, WIN - 1), 0, 1 << 20) * WIN + offsets
    ranking = jnp.where(block_col - offsets >= 0, ranking, (1 << 30) + offsets)
    ordered = (jnp.argsort(ranking, axis=1) + 1).astype(jnp.int32)
    wanted = jax.random.randint(second_key, (NB,), 1, KMAX + 1)
    wanted = jnp.where(jnp.arange(NB) == NB - 1, KMAX, wanted)
    usable = jnp.minimum(wanted, jnp.minimum(jnp.arange(NB) + 1, WIN)).astype(jnp.int32)
    slot_ids = jnp.arange(1, KMAX, dtype=jnp.int32)[None, :]
    picked = block_col - ordered[:, :KMAX - 1]
    tail_part = jnp.where(slot_ids < usable[:, None], picked, -1)
    listing = jnp.concatenate([block_col, tail_part], axis=1).astype(jnp.int32)
    return (listing, usable)


def draw_adjacency(key, part):
    listing, usable = relation(key)
    return listing


def draw_counts(key, part):
    listing, usable = relation(key)
    return usable


def steps_of(stream_key, shape, shards, low, largest):
    def one(position, parts):
        steps = jax.random.uniform(jax.random.fold_in(jax.random.fold_in(stream_key, 6), position), (parts,), jnp.float32, low / len(shards), largest / len(shards))
        return jnp.repeat(jnp.exp(steps), shape[position] // parts).reshape((-1,) + (1,) * (len(shape) - position - 1))

    loudness = one(*shards[0])
    for cut in shards[1:]:
        loudness = loudness * one(*cut)
    return loudness


def noise(stream_key, extent, spread, most, cuts=(), kind=jnp.bfloat16):
    array = spread * jax.random.normal(stream_key, extent, jnp.float32)
    if cuts:
        array = array * steps_of(stream_key, extent, cuts, -0.22, 0.18)
    return jnp.clip(array, -most, most).astype(kind)


def setup_inputs(seed: int = 0) -> dict:
    splits = jax.random.split(jax.random.key(seed), 6)
    queries = draw_queries(jax.random.fold_in(splits[5], 71), 0)
    keys = draw_keys(jax.random.fold_in(splits[5], 71), 0)
    values = noise(splits[2], (TOKENS, H * DH), 1.0, 6.0, ((0, 512),))
    adjacency = draw_adjacency(jax.random.fold_in(splits[5], 71), 0)
    counts = draw_counts(jax.random.fold_in(splits[5], 71), 0)
    return {"queries": queries, "keys": keys, "values": values, "adjacency": adjacency, "counts": counts}


NEG_FILL = -1e+30

def reference(queries, keys, values, adjacency, counts):
    scaling = 1.0 / math.sqrt(DH)
    highest_prec = lax.Precision.HIGHEST
    key_blocks = keys.reshape(NB, BLK, H, DH)
    value_blocks = values.reshape(NB, BLK, H, DH)
    query_blocks = queries.reshape(NB, BLK, H, DH)
    classes = jnp.arange(N_KA, dtype=jnp.int32)
    token_pos = jnp.arange(BLK, dtype=jnp.int32)
    slot_ids = jnp.arange(KMAX, dtype=jnp.int32)

    def one_block(block_id):
        listed = adjacency[block_id].astype(jnp.int32)
        usable = slot_ids < counts[block_id]
        chosen = jnp.where(usable, listed, 0).astype(jnp.int32)
        q_rows = query_blocks[block_id].astype(jnp.float32)
        k_rows = key_blocks[chosen].astype(jnp.float32)
        v_rows = value_blocks[chosen].astype(jnp.float32)
        scores = jnp.einsum('thd,cuhd->htcu', q_rows, k_rows, precision=highest_prec) * scaling
        diagonal = listed == block_id
        allowed = usable[None, :, None] & (jnp.logical_not(diagonal)[None, :, None] | (token_pos[None, None, :] <= token_pos[:, None, None]))
        member = ((chosen % N_KA)[None, :] == classes[:, None]) & usable[None, :]
        masked = jnp.where(allowed[None], scores, NEG_FILL)
        block_max = lax.optimization_barrier(jnp.max(masked, axis=3))
        class_max = lax.optimization_barrier(jnp.max(jnp.where(member[None, None], block_max[:, :, None, :], NEG_FILL), axis=3))
        shared_max = lax.optimization_barrier(jnp.max(jnp.where(member[None, None], class_max[:, :, :, None], NEG_FILL), axis=2))
        weights = jnp.where(allowed[None], jnp.exp(masked - shared_max[..., None]), 0.0)
        block_total = lax.optimization_barrier(jnp.sum(weights, axis=3))
        class_total = lax.optimization_barrier(jnp.sum(jnp.where(member[None, None], block_total[:, :, None, :], 0.0), axis=3))
        rounded = lax.optimization_barrier(weights.astype(jnp.bfloat16)).astype(jnp.float32)
        contrib = jnp.einsum('htcu,cuhd->cthd', rounded, v_rows, precision=highest_prec)
        class_part = jnp.einsum('rc,cthd->rthd', member.astype(jnp.float32), contrib, precision=highest_prec)
        class_part = lax.optimization_barrier(class_part.astype(jnp.bfloat16)).astype(jnp.float32)
        top_score = lax.optimization_barrier(jnp.max(class_max, axis=2))
        factor = jnp.exp(class_max - top_score[..., None])
        denominator = lax.optimization_barrier(jnp.sum(factor * class_total, axis=2))
        numerator = jnp.einsum('htr,rthd->thd', factor, class_part, precision=highest_prec)
        return (numerator / jnp.transpose(denominator)[:, :, None]).reshape(BLK, H * DH).astype(jnp.bfloat16)
    blocks_out = lax.map(one_block, jnp.arange(NB, dtype=jnp.int32))
    return blocks_out.reshape(TOKENS, H * DH)
```

```python
import math

import jax
import jax.numpy as jnp
from jax import lax
from jax.sharding import PartitionSpec as P

DH = 128


NEG_FILL = -1e30


def passed_along(block, axis, distance):
    devices = range(lax.axis_size(axis))
    route = [(i - distance, i) for i in devices if i - distance in devices]
    return lax.ppermute(block, axis, route)


def tile_partials(query_rows, permitted, position, anchors, kv_window, current):
    sources, item_count, feature_width = query_rows.shape
    span_count = kv_window.shape[1]
    block_len = kv_window.shape[2]
    head_count = feature_width // DH
    grouped = math.gcd(sources, max(1, 512 // item_count))
    head_step = math.gcd(head_count, 4)
    scaling = 1.0 / math.sqrt(DH)
    key_window = kv_window[0].reshape(span_count, block_len, head_count, DH)
    value_window = kv_window[1].reshape(span_count, block_len, head_count, DH)
    leading = jnp.arange(span_count) == 0
    key_pos = jnp.arange(block_len, dtype=jnp.int32)

    def one_group(pieces):
        q_group, allow_group, pos_group, anchor_group = pieces
        q_group = q_group.reshape(grouped, item_count, head_count, DH)
        causal = key_pos[None, None, None, :] <= pos_group[:, :, None, None]
        own_block = (anchor_group == current)[:, None] & leading[None, :]
        allowed = (allow_group[:, :, :, None] != 0) & (
            jnp.logical_not(own_block)[:, None, :, None] | causal
        )
        part_list = []
        max_list = []
        total_list = []
        for head_lo in range(0, head_count, head_step):
            head_hi = head_lo + head_step
            scores = (
                jnp.einsum(
                    "gthd,auhd->ghtau",
                    q_group[:, :, head_lo:head_hi],
                    key_window[:, :, head_lo:head_hi],
                    preferred_element_type=jnp.float32,
                )
                * scaling
            )
            masked = jnp.where(allowed[:, None], scores, NEG_FILL)
            highest = jnp.max(masked, axis=(3, 4))
            weights = jnp.where(allowed[:, None], jnp.exp(masked - highest[..., None, None]), 0.0)
            total_list.append(jnp.sum(weights, axis=(3, 4)))
            max_list.append(highest)
            blended = jnp.einsum(
                "ghtau,auhd->gthd",
                weights.astype(jnp.bfloat16),
                value_window[:, :, head_lo:head_hi],
                preferred_element_type=jnp.float32,
            )
            part_list.append(blended.astype(jnp.bfloat16))
        partial_out = jnp.concatenate(part_list, axis=2).reshape(grouped, item_count, feature_width)
        class_max = jnp.transpose(jnp.concatenate(max_list, axis=1), (0, 2, 1))
        class_total = jnp.transpose(jnp.concatenate(total_list, axis=1), (0, 2, 1))
        return (partial_out, class_max, class_total)

    outer = sources // grouped
    reshaped = (
        query_rows.reshape(outer, grouped, item_count, feature_width),
        permitted.reshape(outer, grouped, item_count, span_count),
        position.reshape(outer, grouped, item_count),
        anchors.reshape(outer, grouped),
    )
    partial_out, class_max, class_total = lax.map(one_group, reshaped)
    return (
        partial_out.reshape(sources, item_count, feature_width),
        class_max.reshape(sources, item_count, head_count),
        class_total.reshape(sources, item_count, head_count),
    )


def merge_classes(partial_out, class_max, class_total):
    sources, block_len, feature_width = partial_out.shape
    head_count = class_max.shape[2]
    highest = jnp.max(class_max, axis=0)
    factor = jnp.exp(class_max - highest[None])
    denominator = jnp.sum(factor * class_total, axis=0)
    numerator = jnp.sum(
        factor[..., None] * partial_out.reshape(sources, block_len, head_count, DH), axis=0
    )
    return (
        (numerator / denominator[..., None]).reshape(block_len, feature_width).astype(jnp.bfloat16)
    )


def per_device(queries, keys, values, adjacency, counts):
    block_len, feature_width = queries.shape
    stripe_count = lax.axis_size("ka")
    current = lax.axis_index("ka")
    row_index = lax.axis_index("pb")
    stacked = jnp.stack([keys, values])
    window = [stacked]
    earlier = stacked
    for repeat in range(2):
        earlier = passed_along(earlier, "pb", 1)
        window.append(earlier)
    kv_window = jnp.stack(window, axis=1)
    span_count = len(window)
    lag_ids = jnp.arange(span_count, dtype=jnp.int32)
    slot_ids = jnp.arange(adjacency.shape[1], dtype=jnp.int32)
    positions = jnp.broadcast_to(
        jnp.arange(block_len, dtype=jnp.int32)[None, :], (stripe_count, block_len)
    )
    anchors = jnp.arange(stripe_count, dtype=jnp.int32)
    row_q = lax.all_gather(queries, "ka", axis=0, tiled=True)
    row_table = lax.all_gather(
        jnp.concatenate([adjacency, counts[:, None]], axis=1), "ka", axis=0, tiled=True
    )
    row_adj, row_cnt = row_table[:, :-1], row_table[:, -1]
    wanted = (row_index - lag_ids) * stripe_count + current
    listed = (row_adj[:, None, :] == wanted[None, :, None]) & (
        slot_ids[None, None, :] < row_cnt[:, None, None]
    )
    present = jnp.any(listed, axis=2).astype(jnp.int32)
    permitted = jnp.broadcast_to(present[:, None, :], (stripe_count, block_len, span_count))
    partial_out, class_max, class_total = tile_partials(
        row_q.reshape(stripe_count, block_len, feature_width),
        permitted,
        positions,
        anchors,
        kv_window,
        current,
    )
    partial_out, class_max, class_total = (
        lax.all_to_all(partial_out, "ka", split_axis=0, concat_axis=0, tiled=True),
        lax.all_to_all(class_max, "ka", split_axis=0, concat_axis=0, tiled=True),
        lax.all_to_all(class_total, "ka", split_axis=0, concat_axis=0, tiled=True),
    )
    return merge_classes(partial_out.astype(jnp.float32), class_max, class_total)


def solution(mesh):
    in_specs = (
        P(("pb", "ka"), None),
        P(("pb", "ka"), None),
        P(("pb", "ka"), None),
        P(("pb", "ka"), None),
        P(("pb", "ka")),
    )
    out_specs = P(("pb", "ka"), None)
    return jax.shard_map(
        per_device, mesh=mesh, in_specs=in_specs, out_specs=out_specs, check_vma=False
    )
```

```python
import math

import jax
import jax.numpy as jnp
from jax import lax
from jax.experimental import pallas as pl
from jax.experimental.pallas import tpu as pltpu
from jax.sharding import PartitionSpec as P

DH = 128


NEG_FILL = -1e30
LAGS = 3


def passed_along(block, axis, distance):
    devices = range(lax.axis_size(axis))
    route = [(i - distance, i) for i in devices if i - distance in devices]
    return lax.ppermute(block, axis, route)


def class_kernel(info_ref, q_ref, k1_ref, kx_ref, v1_ref, vx_ref, out_ref, max_ref, tot_ref):
    cp = pl.program_id(0)
    current = info_ref[0]
    block_len = q_ref.shape[1]
    head_count = q_ref.shape[2] // DH
    lag_x = jnp.where(current <= cp, 0, 2)
    listed_1 = info_ref[1 + cp * LAGS + 1] != 0
    listed_x = info_ref[1 + cp * LAGS + lag_x] != 0
    diagonal = current == cp
    reach_1 = jnp.where(listed_1, block_len, -2 * block_len)
    reach_x = jnp.where(listed_x, jnp.where(diagonal, 0, block_len), -2 * block_len)
    q_pos = lax.broadcasted_iota(jnp.int32, (block_len, block_len), 0)
    k_pos = lax.broadcasted_iota(jnp.int32, (block_len, block_len), 1)
    allowed_1 = k_pos <= q_pos + reach_1
    allowed_x = k_pos <= q_pos + reach_x
    scaling = 1.0 / math.sqrt(DH)
    nt = (((1,), (1,)), ((), ()))
    for h in range(head_count):
        cols = slice(h * DH, (h + 1) * DH)
        q = q_ref[0, :, cols]
        s1 = lax.dot_general(q, k1_ref[0, :, cols], nt, preferred_element_type=jnp.float32)
        sx = lax.dot_general(q, kx_ref[0, :, cols], nt, preferred_element_type=jnp.float32)
        s1 = jnp.where(allowed_1, s1 * scaling, NEG_FILL)
        sx = jnp.where(allowed_x, sx * scaling, NEG_FILL)
        highest = jnp.maximum(
            jnp.max(s1, axis=1, keepdims=True), jnp.max(sx, axis=1, keepdims=True)
        )
        w1 = jnp.where(allowed_1, jnp.exp(s1 - highest), 0.0)
        wx = jnp.where(allowed_x, jnp.exp(sx - highest), 0.0)
        total = jnp.sum(w1, axis=1, keepdims=True) + jnp.sum(wx, axis=1, keepdims=True)
        blended = jnp.dot(
            w1.astype(jnp.bfloat16), v1_ref[0, :, cols], preferred_element_type=jnp.float32
        ) + jnp.dot(wx.astype(jnp.bfloat16), vx_ref[0, :, cols], preferred_element_type=jnp.float32)
        out_ref[0, :, cols] = blended.astype(jnp.bfloat16)
        max_ref[0, :, h : h + 1] = highest
        tot_ref[0, :, h : h + 1] = total


def class_partials(info, row_q, key_window, value_window):
    sources, block_len, feature_width = row_q.shape
    head_count = feature_width // DH

    def lag_x_map(cp, info_ref):
        return (jnp.where(info_ref[0] <= cp, 0, 2), 0, 0)

    block = (1, block_len, feature_width)
    stat = (1, block_len, head_count)
    grid_spec = pltpu.PrefetchScalarGridSpec(
        num_scalar_prefetch=1,
        grid=(sources,),
        in_specs=[
            pl.BlockSpec(block, lambda cp, info_ref: (cp, 0, 0)),
            pl.BlockSpec(block, lambda cp, info_ref: (1, 0, 0)),
            pl.BlockSpec(block, lag_x_map),
            pl.BlockSpec(block, lambda cp, info_ref: (1, 0, 0)),
            pl.BlockSpec(block, lag_x_map),
        ],
        out_specs=[
            pl.BlockSpec(block, lambda cp, info_ref: (cp, 0, 0)),
            pl.BlockSpec(stat, lambda cp, info_ref: (cp, 0, 0)),
            pl.BlockSpec(stat, lambda cp, info_ref: (cp, 0, 0)),
        ],
    )
    flops = sources * head_count * 4 * 2 * block_len * block_len * DH
    return pl.pallas_call(
        class_kernel,
        grid_spec=grid_spec,
        out_shape=[
            jax.ShapeDtypeStruct((sources, block_len, feature_width), jnp.bfloat16),
            jax.ShapeDtypeStruct((sources, block_len, head_count), jnp.float32),
            jax.ShapeDtypeStruct((sources, block_len, head_count), jnp.float32),
        ],
        cost_estimate=pl.CostEstimate(
            flops=flops,
            transcendentals=sources * head_count * 2 * block_len * block_len,
            bytes_accessed=2 * sources * block_len * feature_width * 2 + 4 * block_len * feature_width * 2,
        ),
    )(info, row_q, key_window, key_window, value_window, value_window)


def per_device(queries, keys, values, adjacency, counts):
    block_len, feature_width = queries.shape
    head_count = feature_width // DH
    chips = lax.axis_size("z")
    cores = lax.axis_size("core")
    stripe_count = chips * cores
    core = lax.axis_index("core")
    current = lax.axis_index("z") * cores + core
    row_index = lax.axis_index("pb")
    key_window = jnp.stack([keys, passed_along(keys, "pb", 1), passed_along(keys, "pb", 2)])
    value_window = jnp.stack(
        [values, passed_along(values, "pb", 1), passed_along(values, "pb", 2)]
    )
    row_q = lax.all_gather(queries, ("z", "core"), axis=0, tiled=True)
    row_table = lax.all_gather(
        jnp.concatenate([adjacency, counts[:, None]], axis=1), ("z", "core"), axis=0, tiled=True
    )
    row_adj, row_cnt = row_table[:, :-1], row_table[:, -1]
    lag_ids = jnp.arange(LAGS, dtype=jnp.int32)
    slot_ids = jnp.arange(adjacency.shape[1], dtype=jnp.int32)
    wanted = (row_index - lag_ids) * stripe_count + current
    listed = (row_adj[:, None, :] == wanted[None, :, None]) & (
        slot_ids[None, None, :] < row_cnt[:, None, None]
    )
    present = jnp.any(listed, axis=2).astype(jnp.int32)
    info = jnp.concatenate([current.reshape(1).astype(jnp.int32), present.reshape(-1)])
    partial_out, class_max, class_total = class_partials(
        info, row_q.reshape(stripe_count, block_len, feature_width), key_window, value_window
    )

    def split(x):
        x = x.reshape((chips, cores) + x.shape[1:])
        keep = lax.dynamic_index_in_dim(x, core, axis=1, keepdims=False)
        give = lax.dynamic_index_in_dim(x, 1 - core, axis=1, keepdims=False)
        return keep, give

    swap = [(0, 1), (1, 0)]
    own_out, give_out = split(partial_out)
    own_max, give_max = split(class_max)
    own_tot, give_tot = split(class_total)
    peer_out = lax.ppermute(give_out, "core", swap)
    peer_stats = lax.ppermute(jnp.concatenate([give_max, give_tot], axis=2), "core", swap)
    peer_max, peer_tot = peer_stats[..., :head_count], peer_stats[..., head_count:]
    pair_max = jnp.maximum(own_max, peer_max)
    own_f = jnp.exp(own_max - pair_max)
    peer_f = jnp.exp(peer_max - pair_max)
    pair_tot = own_f * own_tot + peer_f * peer_tot
    pair_out = (
        own_f[..., None] * own_out.astype(jnp.float32).reshape(chips, block_len, head_count, DH)
        + peer_f[..., None] * peer_out.astype(jnp.float32).reshape(chips, block_len, head_count, DH)
    ).astype(jnp.bfloat16)

    pair_out = lax.all_to_all(pair_out, "z", split_axis=0, concat_axis=0, tiled=True)
    pair_stats = lax.all_to_all(
        jnp.concatenate([pair_max, pair_tot], axis=2), "z", split_axis=0, concat_axis=0, tiled=True
    )
    pair_max, pair_tot = pair_stats[..., :head_count], pair_stats[..., head_count:]
    highest = jnp.max(pair_max, axis=0)
    factor = jnp.exp(pair_max - highest[None])
    denominator = jnp.sum(factor * pair_tot, axis=0)
    numerator = jnp.sum(factor[..., None] * pair_out.astype(jnp.float32), axis=0)
    return (
        (numerator / denominator[..., None]).reshape(block_len, feature_width).astype(jnp.bfloat16)
    )


def solution(mesh):
    pb, ka = mesh.devices.shape
    grid = jax.sharding.Mesh(mesh.devices.reshape(pb, ka // 2, 2), ("pb", "z", "core"))
    rows = P(("pb", "z", "core"), None)
    in_specs = (rows, rows, rows, rows, P(("pb", "z", "core")))
    return jax.shard_map(
        per_device, mesh=grid, in_specs=in_specs, out_specs=rows, check_vma=False
    )
```

```python
import math

import jax
import jax.numpy as jnp
from jax import lax
from jax.experimental import pallas as pl
from jax.experimental.pallas import tpu as pltpu
from jax.sharding import PartitionSpec as P

DH = 128


NEG_FILL = -1e30
LAGS = 3
CHUNKS = 3


def passed_along(block, axis, distance):
    devices = range(lax.axis_size(axis))
    route = [(i - distance, i) for i in devices if i - distance in devices]
    return lax.ppermute(block, axis, route)


def class_kernel(info_ref, q_ref, k_ref, v_ref, out_ref, stat_ref):
    cp = pl.program_id(0)
    current = info_ref[0]
    block_len = q_ref.shape[0]
    head_count = q_ref.shape[1] // DH
    early = current <= cp
    lag_a = jnp.where(early, 0, 1)
    start = pl.multiple_of(lag_a * block_len, block_len)
    listed_a = info_ref[2 + cp * LAGS + lag_a] != 0
    listed_b = info_ref[3 + cp * LAGS + lag_a] != 0
    diagonal = current == cp
    reach_a = jnp.where(listed_a, jnp.where(diagonal, 0, block_len), -4 * block_len)
    reach_b = jnp.where(listed_b, block_len, -4 * block_len)
    q_pos = lax.broadcasted_iota(jnp.int32, (block_len, 2 * block_len), 0)
    k_pos = lax.broadcasted_iota(jnp.int32, (block_len, 2 * block_len), 1)
    first = k_pos < block_len
    limit = jnp.where(first, q_pos + reach_a, q_pos + (block_len + reach_b))
    allowed = k_pos <= limit
    scaling = 1.0 / math.sqrt(DH)
    nt = (((1,), (1,)), ((), ()))
    for h in range(head_count):
        cols = slice(h * DH, (h + 1) * DH)
        keys = k_ref[pl.ds(start, 2 * block_len), cols]
        scores = lax.dot_general(q_ref[:, cols], keys, nt, preferred_element_type=jnp.float32)
        scores = jnp.where(allowed, scores * scaling, NEG_FILL)
        highest = jnp.max(scores, axis=1, keepdims=True)
        weights = jnp.where(allowed, jnp.exp(scores - highest), 0.0)
        total = jnp.sum(weights, axis=1, keepdims=True)
        blended = jnp.dot(
            weights.astype(jnp.bfloat16),
            v_ref[pl.ds(start, 2 * block_len), cols],
            preferred_element_type=jnp.float32,
        )
        out_ref[0, 0, :, cols] = blended.astype(jnp.bfloat16)
        stat_ref[0, 0, :, h : h + 1] = highest
        stat_ref[0, 0, :, head_count + h : head_count + h + 1] = total


def class_partials(info, row_q, key_window, value_window, chunk, chips, cores):
    block_len = row_q.shape[0] // (chips * cores)
    width = row_q.shape[1]
    head_count = width // DH

    def out_map(cp, info_ref):
        return (jnp.where(cp % cores == info_ref[1], 0, 1), cp // cores, 0, 0)

    window = (key_window.shape[0], width)
    grid_spec = pltpu.PrefetchScalarGridSpec(
        num_scalar_prefetch=1,
        grid=(chips * cores,),
        in_specs=[
            pl.BlockSpec((block_len, width), lambda cp, info_ref: (cp, 0)),
            pl.BlockSpec(window, lambda cp, info_ref: (0, chunk)),
            pl.BlockSpec(window, lambda cp, info_ref: (0, chunk)),
        ],
        out_specs=[
            pl.BlockSpec((1, 1, block_len, width), out_map),
            pl.BlockSpec((1, 1, block_len, 2 * head_count), out_map),
        ],
    )
    sources = chips * cores
    return pl.pallas_call(
        class_kernel,
        grid_spec=grid_spec,
        out_shape=[
            jax.ShapeDtypeStruct((cores, chips, block_len, width), jnp.bfloat16),
            jax.ShapeDtypeStruct((cores, chips, block_len, 2 * head_count), jnp.float32),
        ],
        cost_estimate=pl.CostEstimate(
            flops=sources * head_count * 2 * 2 * block_len * 2 * block_len * DH,
            transcendentals=sources * head_count * 2 * block_len * block_len,
            bytes_accessed=2 * sources * block_len * width * 2 + 4 * 3 * block_len * width * 2,
        ),
    )(info, row_q, key_window, value_window)


def per_device(queries, keys, values, adjacency, counts):
    block_len, feature_width = queries.shape
    chips = lax.axis_size("z")
    cores = lax.axis_size("core")
    stripe_count = chips * cores
    core = lax.axis_index("core")
    current = lax.axis_index("z") * cores + core
    row_index = lax.axis_index("pb")
    stacked = jnp.stack([keys, values])
    lag_1 = passed_along(stacked, "pb", 1)
    lag_2 = passed_along(stacked, "pb", 2)
    key_window = jnp.concatenate([keys, lag_1[0], lag_2[0]], axis=0)
    value_window = jnp.concatenate([values, lag_1[1], lag_2[1]], axis=0)
    row_table = lax.all_gather(
        jnp.concatenate([adjacency, counts[:, None]], axis=1), ("z", "core"), axis=0, tiled=True
    )
    row_adj, row_cnt = row_table[:, :-1], row_table[:, -1]
    lag_ids = jnp.arange(LAGS, dtype=jnp.int32)
    slot_ids = jnp.arange(adjacency.shape[1], dtype=jnp.int32)
    wanted = (row_index - lag_ids) * stripe_count + current
    listed = (row_adj[:, None, :] == wanted[None, :, None]) & (
        slot_ids[None, None, :] < row_cnt[:, None, None]
    )
    present = jnp.any(listed, axis=2).astype(jnp.int32)
    info = jnp.concatenate(
        [jnp.stack([current, core]).astype(jnp.int32), present.reshape(-1)]
    )

    width = feature_width // CHUNKS
    head_count = width // DH
    swap = [(0, 1), (1, 0)]
    finished = []
    for chunk in range(CHUNKS):
        row_q = lax.all_gather(
            queries[:, chunk * width : (chunk + 1) * width], ("z", "core"), axis=0, tiled=True
        )
        partial_out, stats = class_partials(
            info, row_q, key_window, value_window, chunk, chips, cores
        )
        peer_out = lax.ppermute(partial_out[1], "core", swap)
        peer_stats = lax.ppermute(stats[1], "core", swap)
        own_max, own_tot = stats[0, ..., :head_count], stats[0, ..., head_count:]
        peer_max, peer_tot = peer_stats[..., :head_count], peer_stats[..., head_count:]
        pair_max = jnp.maximum(own_max, peer_max)
        own_f = jnp.exp(own_max - pair_max)
        peer_f = jnp.exp(peer_max - pair_max)
        pair_tot = own_f * own_tot + peer_f * peer_tot
        shape = (chips, block_len, head_count, DH)
        pair_out = (
            own_f[..., None] * partial_out[0].astype(jnp.float32).reshape(shape)
            + peer_f[..., None] * peer_out.astype(jnp.float32).reshape(shape)
        ).astype(jnp.bfloat16)
        pair_out = lax.all_to_all(pair_out, "z", split_axis=0, concat_axis=0, tiled=True)
        pair_stats = lax.all_to_all(
            jnp.concatenate([pair_max, pair_tot], axis=2), "z", split_axis=0, concat_axis=0,
            tiled=True,
        )
        pair_max, pair_tot = pair_stats[..., :head_count], pair_stats[..., head_count:]
        highest = jnp.max(pair_max, axis=0)
        factor = jnp.exp(pair_max - highest[None])
        denominator = jnp.sum(factor * pair_tot, axis=0)
        numerator = jnp.sum(factor[..., None] * pair_out.astype(jnp.float32), axis=0)
        finished.append(
            (numerator / denominator[..., None]).reshape(block_len, width).astype(jnp.bfloat16)
        )
    return jnp.concatenate(finished, axis=1)


def solution(mesh):
    pb, ka = mesh.devices.shape
    grid = jax.sharding.Mesh(mesh.devices.reshape(pb, ka // 2, 2), ("pb", "z", "core"))
    rows = P(("pb", "z", "core"), None)
    in_specs = (rows, rows, rows, rows, P(("pb", "z", "core")))
    return jax.shard_map(
        per_device, mesh=grid, in_specs=in_specs, out_specs=rows, check_vma=False
    )
```

```python
import math

import jax
import jax.numpy as jnp
from jax import lax
from jax.experimental import pallas as pl
from jax.experimental.pallas import tpu as pltpu
from jax.sharding import PartitionSpec as P

DH = 128


NEG_FILL = -1e30
LAGS = 3
AXES = ("pb", "z", "core")


def pair_kernel(info_ref, q_ref, k_ref, v_ref, out_ref, stat_ref):
    t = pl.program_id(0)
    chip = info_ref[0]
    core = info_ref[1]
    block_len = out_ref.shape[0]
    head_count = out_ref.shape[1] // DH
    column = 2 * t + core
    q_pos = lax.broadcasted_iota(jnp.int32, (block_len, 2 * block_len), 0)
    k_pos = lax.broadcasted_iota(jnp.int32, (block_len, 2 * block_len), 1)
    first = k_pos < block_len
    starts = []
    masks = []
    for j in range(2):
        key_class = 2 * chip + (core + j) % 2
        lag_a = jnp.where(key_class <= column, 0, 1)
        base = 2 + (t * 2 + j) * LAGS + lag_a
        listed_a = info_ref[base] != 0
        listed_b = info_ref[base + 1] != 0
        diagonal = key_class == column
        reach_a = jnp.where(listed_a, jnp.where(diagonal, 0, block_len), -4 * block_len)
        reach_b = jnp.where(listed_b, block_len, -4 * block_len)
        limit = jnp.where(first, q_pos + reach_a, q_pos + (block_len + reach_b))
        masks.append(k_pos <= limit)
        starts.append(pl.multiple_of(lag_a * block_len, block_len))
    scaling = 1.0 / math.sqrt(DH)
    nt = (((1,), (1,)), ((), ()))
    for h in range(head_count):
        cols = slice(h * DH, (h + 1) * DH)
        q = q_ref[:, cols]
        scores = []
        for j in range(2):
            keys = k_ref[j, pl.ds(starts[j], 2 * block_len), cols]
            s = lax.dot_general(q, keys, nt, preferred_element_type=jnp.float32)
            scores.append(jnp.where(masks[j], s * scaling, NEG_FILL))
        highest = jnp.maximum(
            jnp.max(scores[0], axis=1, keepdims=True), jnp.max(scores[1], axis=1, keepdims=True)
        )
        total = None
        blended = None
        for j in range(2):
            w = jnp.where(masks[j], jnp.exp(scores[j] - highest), 0.0)
            part_total = jnp.sum(w, axis=1, keepdims=True)
            part = jnp.dot(
                w.astype(jnp.bfloat16),
                v_ref[j, pl.ds(starts[j], 2 * block_len), cols],
                preferred_element_type=jnp.float32,
            )
            total = part_total if total is None else total + part_total
            blended = part if blended is None else blended + part
        out_ref[:, cols] = blended.astype(jnp.bfloat16)
        stat_ref[0, :, h : h + 1] = highest
        stat_ref[0, :, head_count + h : head_count + h + 1] = total


def pair_partials(info, row_q, key_window, value_window, feature_width):
    block_len = key_window.shape[1] // LAGS
    sources = row_q.shape[0] // block_len
    head_count = feature_width // DH
    grid_spec = pltpu.PrefetchScalarGridSpec(
        num_scalar_prefetch=1,
        grid=(sources,),
        in_specs=[
            pl.BlockSpec((block_len, row_q.shape[1]), lambda t, info_ref: (t, 0)),
            pl.BlockSpec(key_window.shape, lambda t, info_ref: (0, 0, 0)),
            pl.BlockSpec(value_window.shape, lambda t, info_ref: (0, 0, 0)),
        ],
        out_specs=[
            pl.BlockSpec((block_len, feature_width), lambda t, info_ref: (t, 0)),
            pl.BlockSpec((1, block_len, 2 * head_count), lambda t, info_ref: (t, 0, 0)),
        ],
    )
    return pl.pallas_call(
        pair_kernel,
        grid_spec=grid_spec,
        out_shape=[
            jax.ShapeDtypeStruct((sources * block_len, feature_width), jnp.bfloat16),
            jax.ShapeDtypeStruct((sources, block_len, 2 * head_count), jnp.float32),
        ],
        cost_estimate=pl.CostEstimate(
            flops=sources * head_count * 2 * 2 * 2 * block_len * 2 * block_len * DH,
            transcendentals=sources * head_count * 2 * 2 * block_len * block_len,
            bytes_accessed=2 * sources * block_len * feature_width * 2
            + 2 * 2 * LAGS * block_len * feature_width * 2,
        ),
    )(info, row_q, key_window, value_window)


def per_device(queries, keys, values, adjacency, counts):
    block_len, feature_width = queries.shape
    head_count = feature_width // DH
    rows = lax.axis_size("pb")
    chips = lax.axis_size("z")
    cores = lax.axis_size("core")
    stripe_count = chips * cores
    chip = lax.axis_index("z")
    core = lax.axis_index("core")
    row_index = lax.axis_index("pb")

    stacked = jnp.stack([keys, values])

    def fetched(lag, flip):
        route = []
        for dst in range(rows * stripe_count):
            src_row = dst // stripe_count - lag
            if src_row >= 0:
                route.append((src_row * stripe_count + ((dst % stripe_count) ^ flip), dst))
        return lax.ppermute(stacked, AXES, route)

    own = [stacked, fetched(1, 0), fetched(2, 0)]
    partner = [fetched(0, 1), fetched(1, 1), fetched(2, 1)]
    key_window = jnp.stack(
        [jnp.concatenate([x[0] for x in own]), jnp.concatenate([x[0] for x in partner])]
    )
    value_window = jnp.stack(
        [jnp.concatenate([x[1] for x in own]), jnp.concatenate([x[1] for x in partner])]
    )

    lag_ids = jnp.arange(LAGS, dtype=jnp.int32)
    class_ids = jnp.arange(stripe_count, dtype=jnp.int32)
    slot_ids = jnp.arange(adjacency.shape[1], dtype=jnp.int32)
    wanted = (row_index - lag_ids[None, :]) * stripe_count + class_ids[:, None]
    listed = (adjacency[0][None, None, :] == wanted[:, :, None]) & (
        slot_ids[None, None, :] < counts[0]
    )
    marks = jnp.any(listed, axis=2).reshape(1, -1).astype(jnp.bfloat16)
    spare = jnp.zeros((block_len, DH), jnp.bfloat16)
    spare = lax.dynamic_update_slice(spare, marks, (0, 0))
    row_q = lax.all_gather(
        jnp.concatenate([queries, spare], axis=1), "z", axis=0, tiled=True
    )
    marks_all = row_q.reshape(chips, block_len, -1)[:, 0, feature_width : feature_width + stripe_count * LAGS]
    marks_all = marks_all.reshape(chips, stripe_count, LAGS).astype(jnp.int32)
    mine = [
        lax.dynamic_index_in_dim(marks_all, 2 * chip + (core + j) % 2, axis=1, keepdims=False)
        for j in range(2)
    ]
    info = jnp.concatenate(
        [jnp.stack([chip, core]).astype(jnp.int32), jnp.stack(mine, axis=1).reshape(-1)]
    )

    pair_out, pair_stats = pair_partials(info, row_q, key_window, value_window, feature_width)
    pair_out = lax.all_to_all(
        pair_out.reshape(chips, block_len, head_count, DH), "z", split_axis=0, concat_axis=0,
        tiled=True,
    )
    pair_stats = lax.all_to_all(pair_stats, "z", split_axis=0, concat_axis=0, tiled=True)
    pair_max, pair_tot = pair_stats[..., :head_count], pair_stats[..., head_count:]
    highest = jnp.max(pair_max, axis=0)
    factor = jnp.exp(pair_max - highest[None])
    denominator = jnp.sum(factor * pair_tot, axis=0)
    numerator = jnp.sum(factor[..., None] * pair_out.astype(jnp.float32), axis=0)
    return (
        (numerator / denominator[..., None]).reshape(block_len, feature_width).astype(jnp.bfloat16)
    )


def solution(mesh):
    pb, ka = mesh.devices.shape
    grid = jax.sharding.Mesh(mesh.devices.reshape(pb, ka // 2, 2), AXES)
    rows = P(AXES, None)
    in_specs = (rows, rows, rows, rows, P(AXES))
    return jax.shard_map(
        per_device, mesh=grid, in_specs=in_specs, out_specs=rows, check_vma=False
    )
```

```python
import math

import jax
import jax.numpy as jnp
from jax import lax
from jax.experimental import pallas as pl
from jax.experimental.pallas import tpu as pltpu
from jax.sharding import PartitionSpec as P

DH = 128


NEG_FILL = -1e30
LAGS = 3
AXES = ("pb", "z", "core")


def passed_along(block, axis, distance):
    devices = range(lax.axis_size(axis))
    route = [(i - distance, i) for i in devices if i - distance in devices]
    return lax.ppermute(block, axis, route)


def pair_kernel(info_ref, q_ref, k_ref, v_ref, out_ref, stat_ref):
    t = pl.program_id(0)
    chip = info_ref[0]
    core = info_ref[1]
    block_len = out_ref.shape[0]
    feature_width = k_ref.shape[2]
    head_count = feature_width // DH
    column = 2 * t + core
    q_pos = lax.broadcasted_iota(jnp.int32, (block_len, 2 * block_len), 0)
    k_pos = lax.broadcasted_iota(jnp.int32, (block_len, 2 * block_len), 1)
    first = k_pos < block_len
    starts = []
    masks = []
    stat_ref[...] = jnp.zeros_like(stat_ref)
    for j in range(2):
        key_class = 2 * chip + (core + j) % 2
        lag_a = jnp.where(key_class <= column, 0, 1)
        base = 2 + (t * 2 + j) * LAGS + lag_a
        listed_a = info_ref[base] != 0
        listed_b = info_ref[base + 1] != 0
        diagonal = key_class == column
        reach_a = jnp.where(listed_a, jnp.where(diagonal, 0, block_len), -4 * block_len)
        reach_b = jnp.where(listed_b, block_len, -4 * block_len)
        limit = jnp.where(first, q_pos + reach_a, q_pos + (block_len + reach_b))
        masks.append(k_pos <= limit)
        starts.append(pl.multiple_of(lag_a * block_len, block_len))
    scaling = 1.0 / math.sqrt(DH)
    nt = (((1,), (1,)), ((), ()))
    for h in range(head_count):
        cols = slice(h * DH, (h + 1) * DH)
        q = q_ref[:, cols]
        scores = []
        for j in range(2):
            keys = k_ref[j, pl.ds(starts[j], 2 * block_len), cols]
            s = lax.dot_general(q, keys, nt, preferred_element_type=jnp.float32)
            scores.append(jnp.where(masks[j], s * scaling, NEG_FILL))
        highest = jnp.maximum(
            jnp.max(scores[0], axis=1, keepdims=True), jnp.max(scores[1], axis=1, keepdims=True)
        )
        highest = (highest + jnp.abs(highest) * (2.0**-7)).astype(jnp.bfloat16).astype(jnp.float32)
        total = None
        blended = None
        for j in range(2):
            w = jnp.where(masks[j], jnp.exp(scores[j] - highest), 0.0)
            part_total = jnp.sum(w, axis=1, keepdims=True)
            part = jnp.dot(
                w.astype(jnp.bfloat16),
                v_ref[j, pl.ds(starts[j], 2 * block_len), cols],
                preferred_element_type=jnp.float32,
            )
            total = part_total if total is None else total + part_total
            blended = part if blended is None else blended + part
        out_ref[:, cols] = blended.astype(jnp.bfloat16)
        stat_ref[:, h : h + 1] = highest
        stat_ref[:, head_count + h : head_count + h + 1] = total
    out_ref[:, feature_width:] = stat_ref[...].astype(jnp.bfloat16)


def pair_partials(info, row_q, key_window, value_window):
    block_len = key_window.shape[1] // LAGS
    sources = row_q.shape[0] // block_len
    feature_width = key_window.shape[2]
    head_count = feature_width // DH
    grid_spec = pltpu.PrefetchScalarGridSpec(
        num_scalar_prefetch=1,
        grid=(sources,),
        in_specs=[
            pl.BlockSpec((block_len, row_q.shape[1]), lambda t, info_ref: (t, 0)),
            pl.BlockSpec(key_window.shape, lambda t, info_ref: (0, 0, 0)),
            pl.BlockSpec(value_window.shape, lambda t, info_ref: (0, 0, 0)),
        ],
        out_specs=pl.BlockSpec((block_len, row_q.shape[1]), lambda t, info_ref: (t, 0)),
        scratch_shapes=[pltpu.VMEM((block_len, row_q.shape[1] - feature_width), jnp.float32)],
    )
    return pl.pallas_call(
        pair_kernel,
        grid_spec=grid_spec,
        out_shape=jax.ShapeDtypeStruct(row_q.shape, jnp.bfloat16),
        cost_estimate=pl.CostEstimate(
            flops=sources * head_count * 2 * 2 * 2 * block_len * 2 * block_len * DH,
            transcendentals=sources * head_count * 2 * 2 * block_len * block_len,
            bytes_accessed=2 * sources * block_len * row_q.shape[1] * 2
            + 2 * 2 * LAGS * block_len * feature_width * 2,
        ),
    )(info, row_q, key_window, value_window)


def per_device(queries, keys, values, adjacency, counts):
    block_len, feature_width = queries.shape
    head_count = feature_width // DH
    rows = lax.axis_size("pb")
    chips = lax.axis_size("z")
    cores = lax.axis_size("core")
    stripe_count = chips * cores
    chip = lax.axis_index("z")
    core = lax.axis_index("core")
    row_index = lax.axis_index("pb")

    stacked = jnp.stack([keys, values])

    swap = [(0, 1), (1, 0)]
    lag_1 = passed_along(stacked, "pb", 1)
    lag_2 = passed_along(stacked, "pb", 2)
    partner_0 = lax.ppermute(stacked, "core", swap)
    partner_12 = lax.ppermute(jnp.stack([lag_1, lag_2]), "core", swap)
    own = [stacked, lag_1, lag_2]
    partner = [partner_0, partner_12[0], partner_12[1]]
    key_window = jnp.stack(
        [jnp.concatenate([x[0] for x in own]), jnp.concatenate([x[0] for x in partner])]
    )
    value_window = jnp.stack(
        [jnp.concatenate([x[1] for x in own]), jnp.concatenate([x[1] for x in partner])]
    )

    lag_ids = jnp.arange(LAGS, dtype=jnp.int32)
    class_ids = jnp.arange(stripe_count, dtype=jnp.int32)
    slot_ids = jnp.arange(adjacency.shape[1], dtype=jnp.int32)
    wanted = (row_index - lag_ids[None, :]) * stripe_count + class_ids[:, None]
    listed = (adjacency[0][None, None, :] == wanted[:, :, None]) & (
        slot_ids[None, None, :] < counts[0]
    )
    marks = jnp.any(listed, axis=2).reshape(1, -1).astype(jnp.bfloat16)
    spare = jnp.zeros((block_len, DH), jnp.bfloat16)
    spare = lax.dynamic_update_slice(spare, marks, (0, 0))
    row_q = lax.all_gather(
        jnp.concatenate([queries, spare], axis=1), "z", axis=0, tiled=True
    )
    marks_all = row_q.reshape(chips, block_len, -1)[:, 0, feature_width : feature_width + stripe_count * LAGS]
    marks_all = marks_all.reshape(chips, stripe_count, LAGS).astype(jnp.int32)
    mine = [
        lax.dynamic_index_in_dim(marks_all, 2 * chip + (core + j) % 2, axis=1, keepdims=False)
        for j in range(2)
    ]
    info = jnp.concatenate(
        [jnp.stack([chip, core]).astype(jnp.int32), jnp.stack(mine, axis=1).reshape(-1)]
    )

    pair_out = pair_partials(info, row_q, key_window, value_window)
    pair_out = lax.all_to_all(
        pair_out.reshape(chips, block_len, -1), "z", split_axis=0, concat_axis=0, tiled=True
    )
    pair_stats = pair_out[..., feature_width : feature_width + 2 * head_count].astype(jnp.float32)
    pair_max, pair_tot = pair_stats[..., :head_count], pair_stats[..., head_count:]
    highest = jnp.max(pair_max, axis=0)
    factor = jnp.exp(pair_max - highest[None])
    denominator = jnp.sum(factor * pair_tot, axis=0)
    partial_out = pair_out[..., :feature_width].reshape(chips, block_len, head_count, DH)
    numerator = jnp.sum(factor[..., None] * partial_out.astype(jnp.float32), axis=0)
    return (
        (numerator / denominator[..., None]).reshape(block_len, feature_width).astype(jnp.bfloat16)
    )


def solution(mesh):
    pb, ka = mesh.devices.shape
    grid = jax.sharding.Mesh(mesh.devices.reshape(pb, ka // 2, 2), AXES)
    rows = P(AXES, None)
    in_specs = (rows, rows, rows, rows, P(AXES))
    return jax.shard_map(
        per_device, mesh=grid, in_specs=in_specs, out_specs=rows, check_vma=False
    )
```

```python
import math

import jax
import jax.numpy as jnp
from jax import lax
from jax.experimental import pallas as pl
from jax.experimental.pallas import tpu as pltpu
from jax.sharding import PartitionSpec as P

DH = 128


NEG_FILL = -1e30
LAGS = 3
AXES = ("pb", "z", "core")
HEADER = 4


def passed_along(block, axis, distance):
    devices = range(lax.axis_size(axis))
    route = [(i - distance, i) for i in devices if i - distance in devices]
    return lax.ppermute(block, axis, route)


def pair_kernel(info_ref, q_ref, k_ref, v_ref, out_ref, stat_ref):
    chip = info_ref[0]
    core = info_ref[1]
    chips = info_ref[2]
    t = (chip + info_ref[3] + pl.program_id(0)) % chips
    block_len = out_ref.shape[1]
    feature_width = k_ref.shape[2]
    head_count = feature_width // DH
    column = 2 * t + core
    q_pos = lax.broadcasted_iota(jnp.int32, (block_len, 2 * block_len), 0)
    k_pos = lax.broadcasted_iota(jnp.int32, (block_len, 2 * block_len), 1)
    first = k_pos < block_len
    starts = []
    masks = []
    stat_ref[...] = jnp.zeros_like(stat_ref)
    for j in range(2):
        key_class = 2 * chip + (core + j) % 2
        lag_a = jnp.where(key_class <= column, 0, 1)
        base = HEADER + (t * 2 + j) * LAGS + lag_a
        listed_a = info_ref[base] != 0
        listed_b = info_ref[base + 1] != 0
        diagonal = key_class == column
        reach_a = jnp.where(listed_a, jnp.where(diagonal, 0, block_len), -4 * block_len)
        reach_b = jnp.where(listed_b, block_len, -4 * block_len)
        limit = jnp.where(first, q_pos + reach_a, q_pos + (block_len + reach_b))
        masks.append(k_pos <= limit)
        starts.append(pl.multiple_of(lag_a * block_len, block_len))
    scaling = 1.0 / math.sqrt(DH)
    nt = (((1,), (1,)), ((), ()))
    for h in range(head_count):
        cols = slice(h * DH, (h + 1) * DH)
        q = q_ref[:, cols]
        scores = []
        for j in range(2):
            keys = k_ref[j, pl.ds(starts[j], 2 * block_len), cols]
            s = lax.dot_general(q, keys, nt, preferred_element_type=jnp.float32)
            scores.append(jnp.where(masks[j], s * scaling, NEG_FILL))
        highest = jnp.maximum(
            jnp.max(scores[0], axis=1, keepdims=True), jnp.max(scores[1], axis=1, keepdims=True)
        )
        highest = (highest + jnp.abs(highest) * (2.0**-7)).astype(jnp.bfloat16).astype(jnp.float32)
        total = None
        blended = None
        for j in range(2):
            w = jnp.where(masks[j], jnp.exp(scores[j] - highest), 0.0)
            part_total = jnp.sum(w, axis=1, keepdims=True)
            part = jnp.dot(
                w.astype(jnp.bfloat16),
                v_ref[j, pl.ds(starts[j], 2 * block_len), cols],
                preferred_element_type=jnp.float32,
            )
            total = part_total if total is None else total + part_total
            blended = part if blended is None else blended + part
        out_ref[0, :, cols] = blended.astype(jnp.bfloat16)
        upper = total.astype(jnp.bfloat16).astype(jnp.float32)
        stat_ref[:, h : h + 1] = highest
        stat_ref[:, head_count + h : head_count + h + 1] = upper
        stat_ref[:, 2 * head_count + h : 2 * head_count + h + 1] = total - upper
    out_ref[0, :, feature_width:] = stat_ref[...].astype(jnp.bfloat16)


def pair_partials(info, row_q, key_window, value_window, steps):
    block_len = key_window.shape[1] // LAGS
    chips = row_q.shape[0] // block_len
    feature_width = key_window.shape[2]
    head_count = feature_width // DH

    def q_map(i, info_ref):
        return ((info_ref[0] + info_ref[3] + i) % chips, 0)

    grid_spec = pltpu.PrefetchScalarGridSpec(
        num_scalar_prefetch=1,
        grid=(steps,),
        in_specs=[
            pl.BlockSpec((block_len, row_q.shape[1]), q_map),
            pl.BlockSpec(key_window.shape, lambda i, info_ref: (0, 0, 0)),
            pl.BlockSpec(value_window.shape, lambda i, info_ref: (0, 0, 0)),
        ],
        out_specs=pl.BlockSpec((1, block_len, row_q.shape[1]), lambda i, info_ref: (i, 0, 0)),
        scratch_shapes=[pltpu.VMEM((block_len, row_q.shape[1] - feature_width), jnp.float32)],
    )
    return pl.pallas_call(
        pair_kernel,
        grid_spec=grid_spec,
        out_shape=jax.ShapeDtypeStruct((steps, block_len, row_q.shape[1]), jnp.bfloat16),
        cost_estimate=pl.CostEstimate(
            flops=steps * head_count * 2 * 2 * 2 * block_len * 2 * block_len * DH,
            transcendentals=steps * head_count * 2 * 2 * block_len * block_len,
            bytes_accessed=2 * steps * block_len * row_q.shape[1] * 2
            + 2 * 2 * LAGS * block_len * feature_width * 2,
        ),
    )(info, row_q, key_window, value_window)


def per_device(queries, keys, values, adjacency, counts):
    block_len, feature_width = queries.shape
    head_count = feature_width // DH
    rows = lax.axis_size("pb")
    chips = lax.axis_size("z")
    cores = lax.axis_size("core")
    stripe_count = chips * cores
    chip = lax.axis_index("z")
    core = lax.axis_index("core")
    row_index = lax.axis_index("pb")

    stacked = jnp.stack([keys, values])

    swap = [(0, 1), (1, 0)]
    lag_1 = passed_along(stacked, "pb", 1)
    lag_2 = passed_along(stacked, "pb", 2)
    partner_0 = lax.ppermute(stacked, "core", swap)
    partner_12 = lax.ppermute(jnp.stack([lag_1, lag_2]), "core", swap)
    own = [stacked, lag_1, lag_2]
    partner = [partner_0, partner_12[0], partner_12[1]]
    key_window = jnp.stack(
        [jnp.concatenate([x[0] for x in own]), jnp.concatenate([x[0] for x in partner])]
    )
    value_window = jnp.stack(
        [jnp.concatenate([x[1] for x in own]), jnp.concatenate([x[1] for x in partner])]
    )

    lag_ids = jnp.arange(LAGS, dtype=jnp.int32)
    class_ids = jnp.arange(stripe_count, dtype=jnp.int32)
    slot_ids = jnp.arange(adjacency.shape[1], dtype=jnp.int32)
    wanted = (row_index - lag_ids[None, :]) * stripe_count + class_ids[:, None]
    listed = (adjacency[0][None, None, :] == wanted[:, :, None]) & (
        slot_ids[None, None, :] < counts[0]
    )
    marks = jnp.any(listed, axis=2).reshape(1, -1).astype(jnp.bfloat16)
    spare = jnp.zeros((block_len, DH), jnp.bfloat16)
    spare = lax.dynamic_update_slice(spare, marks, (0, 0))
    row_q = lax.all_gather(
        jnp.concatenate([queries, spare], axis=1), "z", axis=0, tiled=True
    )
    marks_all = row_q.reshape(chips, block_len, -1)[:, 0, feature_width : feature_width + stripe_count * LAGS]
    marks_all = marks_all.reshape(chips, stripe_count, LAGS).astype(jnp.int32)
    mine = [
        lax.dynamic_index_in_dim(marks_all, 2 * chip + (core + j) % 2, axis=1, keepdims=False)
        for j in range(2)
    ]
    mine = jnp.stack(mine, axis=1).reshape(-1)
    header = jnp.stack([chip, core, jnp.int32(chips)]).astype(jnp.int32)

    half = chips // 2
    first_offset = chips // 4
    received = []
    for offset in (first_offset, first_offset + half):
        info = jnp.concatenate([header, jnp.full((1,), offset % chips, jnp.int32), mine])
        pair_out = pair_partials(info, row_q, key_window, value_window, half)
        for i in range(half):
            shift = (offset + i) % chips
            if shift == 0:
                received.append(pair_out[i])
            else:
                route = [(src, (src + shift) % chips) for src in range(chips)]
                received.append(lax.ppermute(pair_out[i], "z", route))
    pair_out = jnp.stack(received)
    pair_stats = pair_out[..., feature_width : feature_width + 3 * head_count].astype(jnp.float32)
    pair_max = pair_stats[..., :head_count]
    pair_tot = pair_stats[..., head_count : 2 * head_count] + pair_stats[..., 2 * head_count :]
    highest = jnp.max(pair_max, axis=0)
    factor = jnp.exp(pair_max - highest[None])
    denominator = jnp.sum(factor * pair_tot, axis=0)
    partial_out = pair_out[..., :feature_width].reshape(chips, block_len, head_count, DH)
    numerator = jnp.sum(factor[..., None] * partial_out.astype(jnp.float32), axis=0)
    return (
        (numerator / denominator[..., None]).reshape(block_len, feature_width).astype(jnp.bfloat16)
    )


def solution(mesh):
    pb, ka = mesh.devices.shape
    grid = jax.sharding.Mesh(mesh.devices.reshape(pb, ka // 2, 2), AXES)
    rows = P(AXES, None)
    in_specs = (rows, rows, rows, rows, P(AXES))
    return jax.shard_map(
        per_device, mesh=grid, in_specs=in_specs, out_specs=rows, check_vma=False
    )
```

```python
import math

import jax
import jax.numpy as jnp
from jax import lax
from jax.experimental import pallas as pl
from jax.experimental.pallas import tpu as pltpu
from jax.sharding import PartitionSpec as P

DH = 128


NEG_FILL = -1e30
LAGS = 3
AXES = ("pb", "z", "core")


def passed_along(block, axis, distance):
    devices = range(lax.axis_size(axis))
    route = [(i - distance, i) for i in devices if i - distance in devices]
    return lax.ppermute(block, axis, route)


def split_parts(value, count):
    parts = []
    for _ in range(count - 1):
        upper = value.astype(jnp.bfloat16).astype(jnp.float32)
        parts.append(upper)
        value = value - upper
    return parts + [value]


def joined(parts, head_count):
    total = parts[..., :head_count]
    for part in range(1, parts.shape[-1] // head_count):
        total = total + parts[..., part * head_count : (part + 1) * head_count]
    return total


def pair_kernel(info_ref, q_ref, k_ref, v_ref, out_ref, stat_ref):
    t = pl.program_id(0)
    chip = info_ref[0]
    core = info_ref[1]
    block_len = out_ref.shape[0]
    feature_width = k_ref.shape[2]
    head_count = feature_width // DH
    column = 2 * t + core
    q_pos = lax.broadcasted_iota(jnp.int32, (block_len, 2 * block_len), 0)
    k_pos = lax.broadcasted_iota(jnp.int32, (block_len, 2 * block_len), 1)
    first = k_pos < block_len
    starts = []
    masks = []
    stat_ref[...] = jnp.zeros_like(stat_ref)
    for j in range(2):
        key_class = 2 * chip + (core + j) % 2
        lag_a = jnp.where(key_class <= column, 0, 1)
        base = 2 + (t * 2 + j) * LAGS + lag_a
        listed_a = info_ref[base] != 0
        listed_b = info_ref[base + 1] != 0
        diagonal = key_class == column
        reach_a = jnp.where(listed_a, jnp.where(diagonal, 0, block_len), -4 * block_len)
        reach_b = jnp.where(listed_b, block_len, -4 * block_len)
        limit = jnp.where(first, q_pos + reach_a, q_pos + (block_len + reach_b))
        masks.append(k_pos <= limit)
        starts.append(pl.multiple_of(lag_a * block_len, block_len))
    scaling = 1.0 / math.sqrt(DH)
    nt = (((1,), (1,)), ((), ()))
    for h in range(head_count):
        cols = slice(h * DH, (h + 1) * DH)
        q = q_ref[:, cols]
        scores = []
        for j in range(2):
            keys = k_ref[j, pl.ds(starts[j], 2 * block_len), cols]
            s = lax.dot_general(q, keys, nt, preferred_element_type=jnp.float32)
            scores.append(jnp.where(masks[j], s * scaling, NEG_FILL))
        highest = jnp.maximum(
            jnp.max(scores[0], axis=1, keepdims=True), jnp.max(scores[1], axis=1, keepdims=True)
        )
        total = None
        blended = None
        for j in range(2):
            w = jnp.where(masks[j], jnp.exp(scores[j] - highest), 0.0)
            part_total = jnp.sum(w, axis=1, keepdims=True)
            part = jnp.dot(
                w.astype(jnp.bfloat16),
                v_ref[j, pl.ds(starts[j], 2 * block_len), cols],
                preferred_element_type=jnp.float32,
            )
            total = part_total if total is None else total + part_total
            blended = part if blended is None else blended + part
        out_ref[:, cols] = blended.astype(jnp.bfloat16)
        for part, value in enumerate(split_parts(highest, 3) + split_parts(total, 2)):
            stat_ref[:, part * head_count + h : part * head_count + h + 1] = value
    out_ref[:, feature_width:] = stat_ref[...].astype(jnp.bfloat16)


def pair_partials(info, row_q, key_window, value_window):
    block_len = key_window.shape[1] // LAGS
    sources = row_q.shape[0] // block_len
    feature_width = key_window.shape[2]
    head_count = feature_width // DH
    grid_spec = pltpu.PrefetchScalarGridSpec(
        num_scalar_prefetch=1,
        grid=(sources,),
        in_specs=[
            pl.BlockSpec((block_len, row_q.shape[1]), lambda t, info_ref: (t, 0)),
            pl.BlockSpec(key_window.shape, lambda t, info_ref: (0, 0, 0)),
            pl.BlockSpec(value_window.shape, lambda t, info_ref: (0, 0, 0)),
        ],
        out_specs=pl.BlockSpec((block_len, row_q.shape[1]), lambda t, info_ref: (t, 0)),
        scratch_shapes=[pltpu.VMEM((block_len, row_q.shape[1] - feature_width), jnp.float32)],
    )
    return pl.pallas_call(
        pair_kernel,
        grid_spec=grid_spec,
        out_shape=jax.ShapeDtypeStruct(row_q.shape, jnp.bfloat16),
        cost_estimate=pl.CostEstimate(
            flops=sources * head_count * 2 * 2 * 2 * block_len * 2 * block_len * DH,
            transcendentals=sources * head_count * 2 * 2 * block_len * block_len,
            bytes_accessed=2 * sources * block_len * row_q.shape[1] * 2
            + 2 * 2 * LAGS * block_len * feature_width * 2,
        ),
    )(info, row_q, key_window, value_window)


def per_device(queries, keys, values, adjacency, counts):
    block_len, feature_width = queries.shape
    head_count = feature_width // DH
    rows = lax.axis_size("pb")
    chips = lax.axis_size("z")
    cores = lax.axis_size("core")
    stripe_count = chips * cores
    chip = lax.axis_index("z")
    core = lax.axis_index("core")
    row_index = lax.axis_index("pb")

    stacked = jnp.stack([keys, values])

    swap = [(0, 1), (1, 0)]
    lag_1 = passed_along(stacked, "pb", 1)
    lag_2 = passed_along(stacked, "pb", 2)
    partner_0 = lax.ppermute(stacked, "core", swap)
    partner_12 = lax.ppermute(jnp.stack([lag_1, lag_2]), "core", swap)
    own = [stacked, lag_1, lag_2]
    partner = [partner_0, partner_12[0], partner_12[1]]
    key_window = jnp.stack(
        [jnp.concatenate([x[0] for x in own]), jnp.concatenate([x[0] for x in partner])]
    )
    value_window = jnp.stack(
        [jnp.concatenate([x[1] for x in own]), jnp.concatenate([x[1] for x in partner])]
    )

    lag_ids = jnp.arange(LAGS, dtype=jnp.int32)
    class_ids = jnp.arange(stripe_count, dtype=jnp.int32)
    slot_ids = jnp.arange(adjacency.shape[1], dtype=jnp.int32)
    wanted = (row_index - lag_ids[None, :]) * stripe_count + class_ids[:, None]
    listed = (adjacency[0][None, None, :] == wanted[:, :, None]) & (
        slot_ids[None, None, :] < counts[0]
    )
    marks = jnp.any(listed, axis=2).reshape(1, -1).astype(jnp.bfloat16)
    spare = jnp.zeros((block_len, DH), jnp.bfloat16)
    spare = lax.dynamic_update_slice(spare, marks, (0, 0))
    row_q = lax.all_gather(
        jnp.concatenate([queries, spare], axis=1), "z", axis=0, tiled=True
    )
    marks_all = row_q.reshape(chips, block_len, -1)[:, 0, feature_width : feature_width + stripe_count * LAGS]
    marks_all = marks_all.reshape(chips, stripe_count, LAGS).astype(jnp.int32)
    mine = [
        lax.dynamic_index_in_dim(marks_all, 2 * chip + (core + j) % 2, axis=1, keepdims=False)
        for j in range(2)
    ]
    info = jnp.concatenate(
        [jnp.stack([chip, core]).astype(jnp.int32), jnp.stack(mine, axis=1).reshape(-1)]
    )

    pair_out = pair_partials(info, row_q, key_window, value_window)
    pair_out = lax.all_to_all(
        pair_out.reshape(chips, block_len, -1), "z", split_axis=0, concat_axis=0, tiled=True
    )
    pair_stats = pair_out[..., feature_width : feature_width + 5 * head_count].astype(jnp.float32)
    pair_max = joined(pair_stats[..., : 3 * head_count], head_count)
    pair_tot = joined(pair_stats[..., 3 * head_count :], head_count)
    highest = jnp.max(pair_max, axis=0)
    factor = jnp.exp(pair_max - highest[None])
    denominator = jnp.sum(factor * pair_tot, axis=0)
    partial_out = pair_out[..., :feature_width].reshape(chips, block_len, head_count, DH)
    numerator = jnp.sum(factor[..., None] * partial_out.astype(jnp.float32), axis=0)
    return (
        (numerator / denominator[..., None]).reshape(block_len, feature_width).astype(jnp.bfloat16)
    )


def solution(mesh):
    pb, ka = mesh.devices.shape
    grid = jax.sharding.Mesh(mesh.devices.reshape(pb, ka // 2, 2), AXES)
    rows = P(AXES, None)
    in_specs = (rows, rows, rows, rows, P(AXES))
    return jax.shard_map(
        per_device, mesh=grid, in_specs=in_specs, out_specs=rows, check_vma=False
    )
```

```python
import math

import jax
import jax.numpy as jnp
from jax import lax
from jax.experimental import pallas as pl
from jax.experimental.pallas import tpu as pltpu
from jax.sharding import PartitionSpec as P

DH = 128


NEG_FILL = -1e30
LAGS = 3
AXES = ("pb", "z", "core")


def passed_along(block, axis, distance):
    devices = range(lax.axis_size(axis))
    route = [(i - distance, i) for i in devices if i - distance in devices]
    return lax.ppermute(block, axis, route)


def split_parts(value, count):
    parts = []
    for _ in range(count - 1):
        upper = value.astype(jnp.bfloat16).astype(jnp.float32)
        parts.append(upper)
        value = value - upper
    return parts + [value]


def joined(parts, head_count):
    total = parts[..., :head_count]
    for part in range(1, parts.shape[-1] // head_count):
        total = total + parts[..., part * head_count : (part + 1) * head_count]
    return total


def pair_kernel(info_ref, q_ref, k_ref, v_ref, out_ref, stat_ref):
    t = pl.program_id(0)
    chip = info_ref[0]
    core = info_ref[1]
    block_len = out_ref.shape[0]
    feature_width = k_ref.shape[2]
    head_count = feature_width // DH
    column = 2 * t + core
    q_pos = lax.broadcasted_iota(jnp.int32, (block_len, 2 * block_len), 0)
    k_pos = lax.broadcasted_iota(jnp.int32, (block_len, 2 * block_len), 1)
    first = k_pos < block_len
    starts = []
    masks = []
    stat_ref[...] = jnp.zeros_like(stat_ref)
    for j in range(2):
        key_class = 2 * chip + (core + j) % 2
        lag_a = jnp.where(key_class <= column, 0, 1)
        base = 2 + (t * 2 + j) * LAGS + lag_a
        listed_a = info_ref[base] != 0
        listed_b = info_ref[base + 1] != 0
        diagonal = key_class == column
        reach_a = jnp.where(listed_a, jnp.where(diagonal, 0, block_len), -4 * block_len)
        reach_b = jnp.where(listed_b, block_len, -4 * block_len)
        limit = jnp.where(first, q_pos + reach_a, q_pos + (block_len + reach_b))
        masks.append(k_pos <= limit)
        starts.append(pl.multiple_of(lag_a * block_len, block_len))
    scaling = 1.0 / math.sqrt(DH)
    nt = (((1,), (1,)), ((), ()))
    for h in range(head_count):
        cols = slice(h * DH, (h + 1) * DH)
        q = q_ref[:, cols]
        scores = []
        for j in range(2):
            keys = k_ref[j, pl.ds(starts[j], 2 * block_len), cols]
            s = lax.dot_general(q, keys, nt, preferred_element_type=jnp.float32)
            scores.append(jnp.where(masks[j], s * scaling, NEG_FILL))
        highest = jnp.maximum(
            jnp.max(scores[0], axis=1, keepdims=True), jnp.max(scores[1], axis=1, keepdims=True)
        )
        total = None
        blended = None
        for j in range(2):
            w = jnp.where(masks[j], jnp.exp(scores[j] - highest), 0.0)
            part_total = jnp.sum(w, axis=1, keepdims=True)
            part = jnp.dot(
                w.astype(jnp.bfloat16),
                v_ref[j, pl.ds(starts[j], 2 * block_len), cols],
                preferred_element_type=jnp.float32,
            )
            total = part_total if total is None else total + part_total
            blended = part if blended is None else blended + part
        out_ref[:, cols] = blended.astype(jnp.bfloat16)
        for part, value in enumerate(split_parts(highest, 3) + split_parts(total, 2)):
            stat_ref[:, part * head_count + h : part * head_count + h + 1] = value
    out_ref[:, feature_width:] = stat_ref[...].astype(jnp.bfloat16)


def pair_partials(info, row_q, key_window, value_window):
    block_len = key_window.shape[1] // LAGS
    sources = row_q.shape[0] // block_len // 2
    feature_width = key_window.shape[2]
    head_count = feature_width // DH
    grid_spec = pltpu.PrefetchScalarGridSpec(
        num_scalar_prefetch=1,
        grid=(sources,),
        in_specs=[
            pl.BlockSpec((block_len, row_q.shape[1]), lambda t, info_ref: (2 * t + info_ref[1], 0)),
            pl.BlockSpec(key_window.shape, lambda t, info_ref: (0, 0, 0)),
            pl.BlockSpec(value_window.shape, lambda t, info_ref: (0, 0, 0)),
        ],
        out_specs=pl.BlockSpec((block_len, row_q.shape[1]), lambda t, info_ref: (t, 0)),
        scratch_shapes=[pltpu.VMEM((block_len, row_q.shape[1] - feature_width), jnp.float32)],
    )
    return pl.pallas_call(
        pair_kernel,
        grid_spec=grid_spec,
        out_shape=jax.ShapeDtypeStruct((sources * block_len, row_q.shape[1]), jnp.bfloat16),
        cost_estimate=pl.CostEstimate(
            flops=sources * head_count * 2 * 2 * 2 * block_len * 2 * block_len * DH,
            transcendentals=sources * head_count * 2 * 2 * block_len * block_len,
            bytes_accessed=2 * sources * block_len * row_q.shape[1] * 2
            + 2 * 2 * LAGS * block_len * feature_width * 2,
        ),
    )(info, row_q, key_window, value_window)


def per_device(queries, keys, values, adjacency, counts):
    block_len, feature_width = queries.shape
    head_count = feature_width // DH
    rows = lax.axis_size("pb")
    chips = lax.axis_size("z")
    cores = lax.axis_size("core")
    stripe_count = chips * cores
    chip = lax.axis_index("z")
    core = lax.axis_index("core")
    row_index = lax.axis_index("pb")

    stacked = jnp.stack([keys, values])

    swap = [(0, 1), (1, 0)]
    lag_1 = passed_along(stacked, "pb", 1)
    lag_2 = passed_along(stacked, "pb", 2)
    partner_0 = lax.ppermute(stacked, "core", swap)
    partner_12 = lax.ppermute(jnp.stack([lag_1, lag_2]), "core", swap)
    own = [stacked, lag_1, lag_2]
    partner = [partner_0, partner_12[0], partner_12[1]]
    key_window = jnp.stack(
        [jnp.concatenate([x[0] for x in own]), jnp.concatenate([x[0] for x in partner])]
    )
    value_window = jnp.stack(
        [jnp.concatenate([x[1] for x in own]), jnp.concatenate([x[1] for x in partner])]
    )

    lag_ids = jnp.arange(LAGS, dtype=jnp.int32)
    class_ids = jnp.arange(stripe_count, dtype=jnp.int32)
    slot_ids = jnp.arange(adjacency.shape[1], dtype=jnp.int32)
    wanted = (row_index - lag_ids[None, :]) * stripe_count + class_ids[:, None]
    listed = (adjacency[0][None, None, :] == wanted[:, :, None]) & (
        slot_ids[None, None, :] < counts[0]
    )
    marks = jnp.any(listed, axis=2).reshape(1, -1).astype(jnp.bfloat16)
    spare = jnp.zeros((block_len, DH), jnp.bfloat16)
    spare = lax.dynamic_update_slice(spare, marks, (0, 0))
    row_q = lax.all_gather(
        jnp.concatenate([queries, spare], axis=1), ("z", "core"), axis=0, tiled=True
    )
    marks_all = row_q.reshape(stripe_count, block_len, -1)[:, 0, feature_width : feature_width + stripe_count * LAGS]
    marks_all = marks_all.reshape(chips, cores, stripe_count, LAGS).astype(jnp.int32)
    marks_all = lax.dynamic_index_in_dim(marks_all, core, axis=1, keepdims=False)
    mine = [
        lax.dynamic_index_in_dim(marks_all, 2 * chip + (core + j) % 2, axis=1, keepdims=False)
        for j in range(2)
    ]
    info = jnp.concatenate(
        [jnp.stack([chip, core]).astype(jnp.int32), jnp.stack(mine, axis=1).reshape(-1)]
    )

    pair_out = pair_partials(info, row_q, key_window, value_window)
    pair_out = lax.all_to_all(
        pair_out.reshape(chips, block_len, -1), "z", split_axis=0, concat_axis=0, tiled=True
    )
    pair_stats = pair_out[..., feature_width : feature_width + 5 * head_count].astype(jnp.float32)
    pair_max = joined(pair_stats[..., : 3 * head_count], head_count)
    pair_tot = joined(pair_stats[..., 3 * head_count :], head_count)
    highest = jnp.max(pair_max, axis=0)
    factor = jnp.exp(pair_max - highest[None])
    denominator = jnp.sum(factor * pair_tot, axis=0)
    partial_out = pair_out[..., :feature_width].reshape(chips, block_len, head_count, DH)
    numerator = jnp.sum(factor[..., None] * partial_out.astype(jnp.float32), axis=0)
    return (
        (numerator / denominator[..., None]).reshape(block_len, feature_width).astype(jnp.bfloat16)
    )


def solution(mesh):
    pb, ka = mesh.devices.shape
    grid = jax.sharding.Mesh(mesh.devices.reshape(pb, ka // 2, 2), AXES)
    rows = P(AXES, None)
    in_specs = (rows, rows, rows, rows, P(AXES))
    return jax.shard_map(
        per_device, mesh=grid, in_specs=in_specs, out_specs=rows, check_vma=False
    )
```

```python
import math

import jax
import jax.numpy as jnp
from jax import lax
from jax.experimental import pallas as pl
from jax.experimental.pallas import tpu as pltpu
from jax.sharding import PartitionSpec as P

DH = 128


NEG_FILL = -1e30
LAGS = 3
AXES = ("pb", "z", "core")


def passed_along(block, axis, distance):
    devices = range(lax.axis_size(axis))
    route = [(i - distance, i) for i in devices if i - distance in devices]
    return lax.ppermute(block, axis, route)


def split_parts(value, count):
    parts = []
    for _ in range(count - 1):
        upper = value.astype(jnp.bfloat16).astype(jnp.float32)
        parts.append(upper)
        value = value - upper
    return parts + [value]


def joined(parts, head_count):
    total = parts[..., :head_count]
    for part in range(1, parts.shape[-1] // head_count):
        total = total + parts[..., part * head_count : (part + 1) * head_count]
    return total


def pair_kernel(info_ref, q_ref, k_ref, v_ref, out_ref, stat_ref):
    t = pl.program_id(0)
    chip = info_ref[0]
    core = info_ref[1]
    block_len = out_ref.shape[0]
    feature_width = k_ref.shape[2]
    head_count = feature_width // DH
    column = 2 * t + core
    q_pos = lax.broadcasted_iota(jnp.int32, (block_len, 2 * block_len), 0)
    k_pos = lax.broadcasted_iota(jnp.int32, (block_len, 2 * block_len), 1)
    first = k_pos < block_len
    starts = []
    masks = []
    stat_ref[...] = jnp.zeros_like(stat_ref)
    for j in range(2):
        key_class = 2 * chip + (core + j) % 2
        lag_a = jnp.where(key_class <= column, 0, 1)
        base = 2 + (t * 2 + j) * LAGS + lag_a
        listed_a = info_ref[base] != 0
        listed_b = info_ref[base + 1] != 0
        diagonal = key_class == column
        reach_a = jnp.where(listed_a, jnp.where(diagonal, 0, block_len), -4 * block_len)
        reach_b = jnp.where(listed_b, block_len, -4 * block_len)
        limit = jnp.where(first, q_pos + reach_a, q_pos + (block_len + reach_b))
        masks.append(k_pos <= limit)
        starts.append(pl.multiple_of(lag_a * block_len, block_len))
    scaling = 1.0 / math.sqrt(DH)
    nt = (((1,), (1,)), ((), ()))
    for h in range(head_count):
        cols = slice(h * DH, (h + 1) * DH)
        q = q_ref[:, cols]
        scores = []
        for j in range(2):
            keys = k_ref[j, pl.ds(starts[j], 2 * block_len), cols]
            s = lax.dot_general(q, keys, nt, preferred_element_type=jnp.float32)
            scores.append(jnp.where(masks[j], s * scaling, NEG_FILL))
        highest = jnp.maximum(
            jnp.max(scores[0], axis=1, keepdims=True), jnp.max(scores[1], axis=1, keepdims=True)
        )
        total = None
        blended = None
        for j in range(2):
            w = jnp.where(masks[j], jnp.exp(scores[j] - highest), 0.0)
            part_total = jnp.sum(w, axis=1, keepdims=True)
            part = jnp.dot(
                w.astype(jnp.bfloat16),
                v_ref[j, pl.ds(starts[j], 2 * block_len), cols],
                preferred_element_type=jnp.float32,
            )
            total = part_total if total is None else total + part_total
            blended = part if blended is None else blended + part
        out_ref[:, cols] = blended.astype(jnp.bfloat16)
        for part, value in enumerate(split_parts(highest, 3) + split_parts(total, 2)):
            stat_ref[:, part * head_count + h : part * head_count + h + 1] = value
    out_ref[:, feature_width:] = stat_ref[...].astype(jnp.bfloat16)


def pair_partials(info, row_q, key_window, value_window):
    block_len = key_window.shape[1] // LAGS
    sources = row_q.shape[0] // block_len
    feature_width = key_window.shape[2]
    head_count = feature_width // DH
    grid_spec = pltpu.PrefetchScalarGridSpec(
        num_scalar_prefetch=1,
        grid=(sources,),
        in_specs=[
            pl.BlockSpec((block_len, row_q.shape[1]), lambda t, info_ref: (t, 0)),
            pl.BlockSpec(key_window.shape, lambda t, info_ref: (0, 0, 0)),
            pl.BlockSpec(value_window.shape, lambda t, info_ref: (0, 0, 0)),
        ],
        out_specs=pl.BlockSpec((block_len, row_q.shape[1]), lambda t, info_ref: (t, 0)),
        scratch_shapes=[pltpu.VMEM((block_len, row_q.shape[1] - feature_width), jnp.float32)],
    )
    return pl.pallas_call(
        pair_kernel,
        grid_spec=grid_spec,
        out_shape=jax.ShapeDtypeStruct(row_q.shape, jnp.bfloat16),
        cost_estimate=pl.CostEstimate(
            flops=sources * head_count * 2 * 2 * 2 * block_len * 2 * block_len * DH,
            transcendentals=sources * head_count * 2 * 2 * block_len * block_len,
            bytes_accessed=2 * sources * block_len * row_q.shape[1] * 2
            + 2 * 2 * LAGS * block_len * feature_width * 2,
        ),
    )(info, row_q, key_window, value_window)


def per_device(queries, keys, values, adjacency, counts):
    block_len, feature_width = queries.shape
    head_count = feature_width // DH
    rows = lax.axis_size("pb")
    chips = lax.axis_size("z")
    cores = lax.axis_size("core")
    stripe_count = chips * cores
    chip = lax.axis_index("z")
    core = lax.axis_index("core")
    row_index = lax.axis_index("pb")

    stacked = jnp.stack([keys, values])

    swap = [(0, 1), (1, 0)]
    lag_1 = passed_along(stacked, "pb", 1)
    lag_2 = passed_along(stacked, "pb", 2)
    partner_0 = lax.ppermute(stacked, "core", swap)
    partner_12 = lax.ppermute(jnp.stack([lag_1, lag_2]), "core", swap)
    own = [stacked, lag_1, lag_2]
    partner = [partner_0, partner_12[0], partner_12[1]]
    key_window = jnp.stack(
        [jnp.concatenate([x[0] for x in own]), jnp.concatenate([x[0] for x in partner])]
    )
    value_window = jnp.stack(
        [jnp.concatenate([x[1] for x in own]), jnp.concatenate([x[1] for x in partner])]
    )

    lag_ids = jnp.arange(LAGS, dtype=jnp.int32)
    class_ids = jnp.arange(stripe_count, dtype=jnp.int32)
    slot_ids = jnp.arange(adjacency.shape[1], dtype=jnp.int32)
    wanted = (row_index - lag_ids[None, :]) * stripe_count + class_ids[:, None]
    listed = (adjacency[0][None, None, :] == wanted[:, :, None]) & (
        slot_ids[None, None, :] < counts[0]
    )
    marks = jnp.any(listed, axis=2).reshape(1, -1).astype(jnp.bfloat16)
    spare = jnp.zeros((block_len, DH), jnp.bfloat16)
    spare = lax.dynamic_update_slice(spare, marks, (0, 0))
    row_q = lax.all_gather(
        jnp.concatenate([queries, spare], axis=1), "z", axis=0, tiled=True
    )
    marks_all = row_q.reshape(chips, block_len, -1)[:, 0, feature_width : feature_width + stripe_count * LAGS]
    marks_all = marks_all.reshape(chips, stripe_count, LAGS).astype(jnp.int32)
    mine = [
        lax.dynamic_index_in_dim(marks_all, 2 * chip + (core + j) % 2, axis=1, keepdims=False)
        for j in range(2)
    ]
    info = jnp.concatenate(
        [jnp.stack([chip, core]).astype(jnp.int32), jnp.stack(mine, axis=1).reshape(-1)]
    )

    pair_out = pair_partials(info, row_q, key_window, value_window)
    pair_out = pair_out.reshape(chips, block_len, -1)

    def decode(block):
        stats = block[:, feature_width : feature_width + 5 * head_count].astype(jnp.float32)
        values = block[:, :feature_width].astype(jnp.float32).reshape(block_len, head_count, DH)
        return values, joined(stats[:, : 3 * head_count], head_count), joined(
            stats[:, 3 * head_count :], head_count
        )

    def merged(blocks):
        decoded = [decode(b) for b in blocks]
        top = decoded[0][1]
        for _, m, _ in decoded[1:]:
            top = jnp.maximum(top, m)
        values = None
        total = None
        for v, m, l in decoded:
            f = jnp.exp(m - top)
            values = f[..., None] * v if values is None else values + f[..., None] * v
            total = f * l if total is None else total + f * l
        return values, top, total

    def encoded(values, top, total):
        parts = split_parts(top, 3) + split_parts(total, 2)
        spare = jnp.zeros((block_len, DH - 5 * head_count), jnp.float32)
        stats = jnp.concatenate(parts + [spare], axis=1)
        return jnp.concatenate(
            [values.reshape(block_len, feature_width), stats], axis=1
        ).astype(jnp.bfloat16)

    def block_for(offset):
        return lax.dynamic_index_in_dim(pair_out, (chip + offset) % chips, axis=0, keepdims=False)

    rightward = [(z, (z + 1) % chips) for z in range(chips)]
    leftward = [(z, (z - 1) % chips) for z in range(chips)]
    reach_r = chips // 2
    reach_l = chips - 1 - reach_r
    acc_r = block_for(reach_r)
    acc_l = block_for(-reach_l)
    for step in range(1, reach_r):
        acc_r = encoded(*merged([lax.ppermute(acc_r, "z", rightward), block_for(reach_r - step)]))
        if step < reach_l:
            acc_l = encoded(
                *merged([lax.ppermute(acc_l, "z", leftward), block_for(step - reach_l)])
            )
    final = [block_for(0), lax.ppermute(acc_r, "z", rightward)]
    if reach_l > 0:
        final.append(lax.ppermute(acc_l, "z", leftward))
    values, top, total = merged(final)
    return (values / total[..., None]).reshape(block_len, feature_width).astype(jnp.bfloat16)


def solution(mesh):
    pb, ka = mesh.devices.shape
    grid = jax.sharding.Mesh(mesh.devices.reshape(pb, ka // 2, 2), AXES)
    rows = P(AXES, None)
    in_specs = (rows, rows, rows, rows, P(AXES))
    return jax.shard_map(
        per_device, mesh=grid, in_specs=in_specs, out_specs=rows, check_vma=False
    )
```

```python
import math

import jax
import jax.numpy as jnp
from jax import lax
from jax.experimental import pallas as pl
from jax.experimental.pallas import tpu as pltpu
from jax.sharding import PartitionSpec as P

DH = 128


NEG_FILL = -1e30
LAGS = 3
AXES = ("pb", "z", "core")
HEADER = 4


def passed_along(block, axis, distance):
    devices = range(lax.axis_size(axis))
    route = [(i - distance, i) for i in devices if i - distance in devices]
    return lax.ppermute(block, axis, route)


def split_parts(value, count):
    parts = []
    for _ in range(count - 1):
        upper = value.astype(jnp.bfloat16).astype(jnp.float32)
        parts.append(upper)
        value = value - upper
    return parts + [value]


def joined(parts, head_count):
    total = parts[..., :head_count]
    for part in range(1, parts.shape[-1] // head_count):
        total = total + parts[..., part * head_count : (part + 1) * head_count]
    return total


def pair_kernel(info_ref, q_ref, k_ref, v_ref, out_ref, stat_ref):
    chip = info_ref[0]
    core = info_ref[1]
    chips = info_ref[2]
    t = (chip + info_ref[info_ref[3] + pl.program_id(0)]) % chips
    block_len = out_ref.shape[1]
    feature_width = k_ref.shape[2]
    head_count = feature_width // DH
    column = 2 * t + core
    q_pos = lax.broadcasted_iota(jnp.int32, (block_len, 2 * block_len), 0)
    k_pos = lax.broadcasted_iota(jnp.int32, (block_len, 2 * block_len), 1)
    first = k_pos < block_len
    starts = []
    masks = []
    stat_ref[...] = jnp.zeros_like(stat_ref)
    for j in range(2):
        key_class = 2 * chip + (core + j) % 2
        lag_a = jnp.where(key_class <= column, 0, 1)
        base = HEADER + (t * 2 + j) * LAGS + lag_a
        listed_a = info_ref[base] != 0
        listed_b = info_ref[base + 1] != 0
        diagonal = key_class == column
        reach_a = jnp.where(listed_a, jnp.where(diagonal, 0, block_len), -4 * block_len)
        reach_b = jnp.where(listed_b, block_len, -4 * block_len)
        limit = jnp.where(first, q_pos + reach_a, q_pos + (block_len + reach_b))
        masks.append(k_pos <= limit)
        starts.append(pl.multiple_of(lag_a * block_len, block_len))
    scaling = 1.0 / math.sqrt(DH)
    nt = (((1,), (1,)), ((), ()))
    for h in range(head_count):
        cols = slice(h * DH, (h + 1) * DH)
        q = q_ref[:, cols]
        scores = []
        for j in range(2):
            keys = k_ref[j, pl.ds(starts[j], 2 * block_len), cols]
            s = lax.dot_general(q, keys, nt, preferred_element_type=jnp.float32)
            scores.append(jnp.where(masks[j], s * scaling, NEG_FILL))
        highest = jnp.maximum(
            jnp.maximum(
                jnp.max(scores[0], axis=1, keepdims=True), jnp.max(scores[1], axis=1, keepdims=True)
            ),
            0.1 * NEG_FILL,
        )
        total = None
        blended = None
        for j in range(2):
            w = jnp.exp(scores[j] - highest)
            part_total = jnp.sum(w, axis=1, keepdims=True)
            part = jnp.dot(
                w.astype(jnp.bfloat16),
                v_ref[j, pl.ds(starts[j], 2 * block_len), cols],
                preferred_element_type=jnp.float32,
            )
            total = part_total if total is None else total + part_total
            blended = part if blended is None else blended + part
        out_ref[0, :, cols] = blended.astype(jnp.bfloat16)
        for part, value in enumerate(split_parts(highest, 3) + split_parts(total, 2)):
            stat_ref[:, part * head_count + h : part * head_count + h + 1] = value
    out_ref[0, :, feature_width:] = stat_ref[...].astype(jnp.bfloat16)


def pair_partials(info, row_q, key_window, value_window, steps):
    block_len = key_window.shape[1] // LAGS
    chips = row_q.shape[0] // block_len
    feature_width = key_window.shape[2]
    head_count = feature_width // DH

    def q_map(i, info_ref):
        return ((info_ref[0] + info_ref[info_ref[3] + i]) % chips, 0)

    grid_spec = pltpu.PrefetchScalarGridSpec(
        num_scalar_prefetch=1,
        grid=(steps,),
        in_specs=[
            pl.BlockSpec((block_len, row_q.shape[1]), q_map),
            pl.BlockSpec(key_window.shape, lambda i, info_ref: (0, 0, 0)),
            pl.BlockSpec(value_window.shape, lambda i, info_ref: (0, 0, 0)),
        ],
        out_specs=pl.BlockSpec((1, block_len, row_q.shape[1]), lambda i, info_ref: (i, 0, 0)),
        scratch_shapes=[pltpu.VMEM((block_len, row_q.shape[1] - feature_width), jnp.float32)],
    )
    return pl.pallas_call(
        pair_kernel,
        grid_spec=grid_spec,
        out_shape=jax.ShapeDtypeStruct((steps, block_len, row_q.shape[1]), jnp.bfloat16),
        cost_estimate=pl.CostEstimate(
            flops=steps * head_count * 2 * 2 * 2 * block_len * 2 * block_len * DH,
            transcendentals=steps * head_count * 2 * 2 * block_len * block_len,
            bytes_accessed=2 * steps * block_len * row_q.shape[1] * 2
            + 2 * 2 * LAGS * block_len * feature_width * 2,
        ),
    )(info, row_q, key_window, value_window)


def per_device(queries, keys, values, adjacency, counts):
    block_len, feature_width = queries.shape
    head_count = feature_width // DH
    rows = lax.axis_size("pb")
    chips = lax.axis_size("z")
    cores = lax.axis_size("core")
    stripe_count = chips * cores
    chip = lax.axis_index("z")
    core = lax.axis_index("core")
    row_index = lax.axis_index("pb")

    stacked = jnp.stack([keys, values])

    swap = [(0, 1), (1, 0)]
    lag_1 = passed_along(stacked, "pb", 1)
    lag_2 = passed_along(stacked, "pb", 2)
    partner_0 = lax.ppermute(stacked, "core", swap)
    partner_12 = lax.ppermute(jnp.stack([lag_1, lag_2]), "core", swap)
    own = [stacked, lag_1, lag_2]
    partner = [partner_0, partner_12[0], partner_12[1]]
    key_window = jnp.stack(
        [jnp.concatenate([x[0] for x in own]), jnp.concatenate([x[0] for x in partner])]
    )
    value_window = jnp.stack(
        [jnp.concatenate([x[1] for x in own]), jnp.concatenate([x[1] for x in partner])]
    )

    lag_ids = jnp.arange(LAGS, dtype=jnp.int32)
    class_ids = jnp.arange(stripe_count, dtype=jnp.int32)
    slot_ids = jnp.arange(adjacency.shape[1], dtype=jnp.int32)
    wanted = (row_index - lag_ids[None, :]) * stripe_count + class_ids[:, None]
    listed = (adjacency[0][None, None, :] == wanted[:, :, None]) & (
        slot_ids[None, None, :] < counts[0]
    )
    marks = jnp.any(listed, axis=2).reshape(1, -1).astype(jnp.bfloat16)
    spare = jnp.zeros((block_len, DH), jnp.bfloat16)
    spare = lax.dynamic_update_slice(spare, marks, (0, 0))
    row_q = lax.all_gather(
        jnp.concatenate([queries, spare], axis=1), "z", axis=0, tiled=True
    )
    marks_all = row_q.reshape(chips, block_len, -1)[:, 0, feature_width : feature_width + stripe_count * LAGS]
    marks_all = marks_all.reshape(chips, stripe_count, LAGS).astype(jnp.int32)
    mine = [
        lax.dynamic_index_in_dim(marks_all, 2 * chip + (core + j) % 2, axis=1, keepdims=False)
        for j in range(2)
    ]
    mine = jnp.stack(mine, axis=1).reshape(-1)
    header = jnp.stack([chip, core, jnp.int32(chips), jnp.int32(HEADER + mine.shape[0])])

    reach_r = chips // 2
    reach_l = chips - 1 - reach_r
    order = []
    for step in range(reach_r + 1):
        order.append(reach_r - step)
        if step < reach_l:
            order.append(step - reach_l)
    blocks = {}

    def compute(offsets, queries_in):
        info = jnp.concatenate(
            [header.astype(jnp.int32), mine, jnp.array(offsets, jnp.int32) % chips]
        )
        out = pair_partials(info, queries_in, key_window, value_window, len(offsets))
        for i, offset in enumerate(offsets):
            blocks[offset] = out[i]

    def decode(block):
        stats = block[:, feature_width : feature_width + 5 * head_count].astype(jnp.float32)
        values = block[:, :feature_width].astype(jnp.float32).reshape(block_len, head_count, DH)
        return values, joined(stats[:, : 3 * head_count], head_count), joined(
            stats[:, 3 * head_count :], head_count
        )

    def merged(blocks):
        decoded = [decode(b) for b in blocks]
        top = decoded[0][1]
        for _, m, _ in decoded[1:]:
            top = jnp.maximum(top, m)
        values = None
        total = None
        for v, m, l in decoded:
            f = jnp.exp(m - top)
            values = f[..., None] * v if values is None else values + f[..., None] * v
            total = f * l if total is None else total + f * l
        return values, top, total

    def encoded(values, top, total):
        parts = split_parts(top, 3) + split_parts(total, 2)
        spare = jnp.zeros((block_len, DH - 5 * head_count), jnp.float32)
        stats = jnp.concatenate(parts + [spare], axis=1)
        return jnp.concatenate(
            [values.reshape(block_len, feature_width), stats], axis=1
        ).astype(jnp.bfloat16)

    def block_for(offset):
        return blocks[offset]

    rightward = [(z, (z + 1) % chips) for z in range(chips)]
    leftward = [(z, (z - 1) % chips) for z in range(chips)]
    compute(order, row_q)
    acc_r = block_for(reach_r)
    acc_l = block_for(-reach_l)
    for step in range(1, reach_r):
        acc_r = encoded(*merged([lax.ppermute(acc_r, "z", rightward), block_for(reach_r - step)]))
        if step < reach_l:
            acc_l = encoded(
                *merged([lax.ppermute(acc_l, "z", leftward), block_for(step - reach_l)])
            )
    final = [block_for(0), lax.ppermute(acc_r, "z", rightward)]
    if reach_l > 0:
        final.append(lax.ppermute(acc_l, "z", leftward))
    values, top, total = merged(final)
    return (values / total[..., None]).reshape(block_len, feature_width).astype(jnp.bfloat16)


def solution(mesh):
    pb, ka = mesh.devices.shape
    grid = jax.sharding.Mesh(mesh.devices.reshape(pb, ka // 2, 2), AXES)
    rows = P(AXES, None)
    in_specs = (rows, rows, rows, rows, P(AXES))
    return jax.shard_map(
        per_device, mesh=grid, in_specs=in_specs, out_specs=rows, check_vma=False
    )
```

```python
import math

import jax
import jax.numpy as jnp
from jax import lax
from jax.experimental import pallas as pl
from jax.experimental.pallas import tpu as pltpu
from jax.sharding import PartitionSpec as P

DH = 128


NEG_FILL = -1e30
LAGS = 3
AXES = ("pb", "z", "core")


def passed_along(block, axis, distance):
    devices = range(lax.axis_size(axis))
    route = [(i - distance, i) for i in devices if i - distance in devices]
    return lax.ppermute(block, axis, route)


def split_parts(value, count):
    parts = []
    for _ in range(count - 1):
        upper = value.astype(jnp.bfloat16).astype(jnp.float32)
        parts.append(upper)
        value = value - upper
    return parts + [value]


def joined(parts, head_count):
    total = parts[..., :head_count]
    for part in range(1, parts.shape[-1] // head_count):
        total = total + parts[..., part * head_count : (part + 1) * head_count]
    return total


def pair_kernel(info_ref, q_ref, k_ref, v_ref, out_ref, stat_ref):
    t = pl.program_id(0)
    chip = info_ref[0]
    core = info_ref[1]
    block_len = out_ref.shape[0]
    feature_width = k_ref.shape[2]
    head_count = feature_width // DH
    column = 2 * t + core
    q_pos = lax.broadcasted_iota(jnp.int32, (block_len, 2 * block_len), 0)
    k_pos = lax.broadcasted_iota(jnp.int32, (block_len, 2 * block_len), 1)
    first = k_pos < block_len
    starts = []
    masks = []
    stat_ref[...] = jnp.zeros_like(stat_ref)
    for j in range(2):
        key_class = 2 * chip + (core + j) % 2
        lag_a = jnp.where(key_class <= column, 0, 1)
        base = 2 + (t * 2 + j) * LAGS + lag_a
        listed_a = info_ref[base] != 0
        listed_b = info_ref[base + 1] != 0
        diagonal = key_class == column
        reach_a = jnp.where(listed_a, jnp.where(diagonal, 0, block_len), -4 * block_len)
        reach_b = jnp.where(listed_b, block_len, -4 * block_len)
        limit = jnp.where(first, q_pos + reach_a, q_pos + (block_len + reach_b))
        masks.append(k_pos <= limit)
        starts.append(pl.multiple_of(lag_a * block_len, block_len))
    scaling = 1.0 / math.sqrt(DH)
    nt = (((1,), (1,)), ((), ()))
    for h in range(head_count):
        cols = slice(h * DH, (h + 1) * DH)
        q = q_ref[:, cols]
        scores = []
        for j in range(2):
            keys = k_ref[j, pl.ds(starts[j], 2 * block_len), cols]
            s = lax.dot_general(q, keys, nt, preferred_element_type=jnp.float32)
            scores.append(jnp.where(masks[j], s * scaling, NEG_FILL))
        highest = jnp.maximum(
            jnp.max(scores[0], axis=1, keepdims=True), jnp.max(scores[1], axis=1, keepdims=True)
        )
        total = None
        blended = None
        for j in range(2):
            w = jnp.where(masks[j], jnp.exp(scores[j] - highest), 0.0)
            part_total = jnp.sum(w, axis=1, keepdims=True)
            part = jnp.dot(
                w.astype(jnp.bfloat16),
                v_ref[j, pl.ds(starts[j], 2 * block_len), cols],
                preferred_element_type=jnp.float32,
            )
            total = part_total if total is None else total + part_total
            blended = part if blended is None else blended + part
        out_ref[:, cols] = blended.astype(jnp.bfloat16)
        for part, value in enumerate(split_parts(highest, 3) + split_parts(total, 2)):
            stat_ref[:, part * head_count + h : part * head_count + h + 1] = value
    out_ref[:, feature_width:] = stat_ref[...].astype(jnp.bfloat16)


def pair_partials(info, row_q, key_window, value_window):
    block_len = key_window.shape[1] // LAGS
    sources = row_q.shape[0] // block_len
    feature_width = key_window.shape[2]
    head_count = feature_width // DH
    grid_spec = pltpu.PrefetchScalarGridSpec(
        num_scalar_prefetch=1,
        grid=(sources,),
        in_specs=[
            pl.BlockSpec(
                (block_len, row_q.shape[1]), lambda t, info_ref: ((t - info_ref[0]) % sources, 0)
            ),
            pl.BlockSpec(key_window.shape, lambda t, info_ref: (0, 0, 0)),
            pl.BlockSpec(value_window.shape, lambda t, info_ref: (0, 0, 0)),
        ],
        out_specs=pl.BlockSpec((block_len, row_q.shape[1]), lambda t, info_ref: (t, 0)),
        scratch_shapes=[pltpu.VMEM((block_len, row_q.shape[1] - feature_width), jnp.float32)],
    )
    return pl.pallas_call(
        pair_kernel,
        grid_spec=grid_spec,
        out_shape=jax.ShapeDtypeStruct(row_q.shape, jnp.bfloat16),
        cost_estimate=pl.CostEstimate(
            flops=sources * head_count * 2 * 2 * 2 * block_len * 2 * block_len * DH,
            transcendentals=sources * head_count * 2 * 2 * block_len * block_len,
            bytes_accessed=2 * sources * block_len * row_q.shape[1] * 2
            + 2 * 2 * LAGS * block_len * feature_width * 2,
        ),
    )(info, row_q, key_window, value_window)


def per_device(queries, keys, values, adjacency, counts):
    block_len, feature_width = queries.shape
    head_count = feature_width // DH
    rows = lax.axis_size("pb")
    chips = lax.axis_size("z")
    cores = lax.axis_size("core")
    stripe_count = chips * cores
    chip = lax.axis_index("z")
    core = lax.axis_index("core")
    row_index = lax.axis_index("pb")

    stacked = jnp.stack([keys, values])

    swap = [(0, 1), (1, 0)]
    lag_1 = passed_along(stacked, "pb", 1)
    lag_2 = passed_along(stacked, "pb", 2)
    partner_0 = lax.ppermute(stacked, "core", swap)
    partner_12 = lax.ppermute(jnp.stack([lag_1, lag_2]), "core", swap)
    own = [stacked, lag_1, lag_2]
    partner = [partner_0, partner_12[0], partner_12[1]]
    key_window = jnp.stack(
        [jnp.concatenate([x[0] for x in own]), jnp.concatenate([x[0] for x in partner])]
    )
    value_window = jnp.stack(
        [jnp.concatenate([x[1] for x in own]), jnp.concatenate([x[1] for x in partner])]
    )

    lag_ids = jnp.arange(LAGS, dtype=jnp.int32)
    class_ids = jnp.arange(stripe_count, dtype=jnp.int32)
    slot_ids = jnp.arange(adjacency.shape[1], dtype=jnp.int32)
    wanted = (row_index - lag_ids[None, :]) * stripe_count + class_ids[:, None]
    listed = (adjacency[0][None, None, :] == wanted[:, :, None]) & (
        slot_ids[None, None, :] < counts[0]
    )
    marks = jnp.any(listed, axis=2).reshape(1, -1).astype(jnp.bfloat16)
    spare = jnp.zeros((block_len, DH), jnp.bfloat16)
    spare = lax.dynamic_update_slice(spare, marks, (0, 0))
    own_q = jnp.concatenate([queries, spare], axis=1)
    rightward = [(z, (z + 1) % chips) for z in range(chips)]
    leftward = [(z, (z - 1) % chips) for z in range(chips)]
    reach_r = chips // 2
    reach_l = chips - 1 - reach_r
    slots = [None] * chips
    slots[0] = own_q
    moving_r = own_q
    moving_l = own_q
    for step in range(1, reach_r + 1):
        moving_r = lax.ppermute(moving_r, "z", rightward)
        slots[(chips - step) % chips] = moving_r
        if step <= reach_l:
            moving_l = lax.ppermute(moving_l, "z", leftward)
            slots[step] = moving_l
    row_q = jnp.concatenate(slots, axis=0)
    marks_rel = row_q.reshape(chips, block_len, -1)[:, 0, feature_width : feature_width + stripe_count * LAGS]
    marks_rel = marks_rel.reshape(chips, stripe_count, LAGS).astype(jnp.int32)
    marks_all = jnp.roll(marks_rel, chip, axis=0)
    mine = [
        lax.dynamic_index_in_dim(marks_all, 2 * chip + (core + j) % 2, axis=1, keepdims=False)
        for j in range(2)
    ]
    info = jnp.concatenate(
        [jnp.stack([chip, core]).astype(jnp.int32), jnp.stack(mine, axis=1).reshape(-1)]
    )

    pair_out = pair_partials(info, row_q, key_window, value_window)
    pair_out = pair_out.reshape(chips, block_len, -1)

    def decode(block):
        stats = block[:, feature_width : feature_width + 5 * head_count].astype(jnp.float32)
        values = block[:, :feature_width].astype(jnp.float32).reshape(block_len, head_count, DH)
        return values, joined(stats[:, : 3 * head_count], head_count), joined(
            stats[:, 3 * head_count :], head_count
        )

    def merged(blocks):
        decoded = [decode(b) for b in blocks]
        top = decoded[0][1]
        for _, m, _ in decoded[1:]:
            top = jnp.maximum(top, m)
        values = None
        total = None
        for v, m, l in decoded:
            f = jnp.exp(m - top)
            values = f[..., None] * v if values is None else values + f[..., None] * v
            total = f * l if total is None else total + f * l
        return values, top, total

    def encoded(values, top, total):
        parts = split_parts(top, 3) + split_parts(total, 2)
        spare = jnp.zeros((block_len, DH - 5 * head_count), jnp.float32)
        stats = jnp.concatenate(parts + [spare], axis=1)
        return jnp.concatenate(
            [values.reshape(block_len, feature_width), stats], axis=1
        ).astype(jnp.bfloat16)

    def block_for(offset):
        return lax.dynamic_index_in_dim(pair_out, (chip + offset) % chips, axis=0, keepdims=False)

    acc_r = block_for(reach_r)
    acc_l = block_for(-reach_l)
    for step in range(1, reach_r):
        acc_r = encoded(*merged([lax.ppermute(acc_r, "z", rightward), block_for(reach_r - step)]))
        if step < reach_l:
            acc_l = encoded(
                *merged([lax.ppermute(acc_l, "z", leftward), block_for(step - reach_l)])
            )
    final = [block_for(0), lax.ppermute(acc_r, "z", rightward)]
    if reach_l > 0:
        final.append(lax.ppermute(acc_l, "z", leftward))
    values, top, total = merged(final)
    return (values / total[..., None]).reshape(block_len, feature_width).astype(jnp.bfloat16)


def solution(mesh):
    pb, ka = mesh.devices.shape
    grid = jax.sharding.Mesh(mesh.devices.reshape(pb, ka // 2, 2), AXES)
    rows = P(AXES, None)
    in_specs = (rows, rows, rows, rows, P(AXES))
    return jax.shard_map(
        per_device, mesh=grid, in_specs=in_specs, out_specs=rows, check_vma=False
    )
```

```python
import math

import jax
import jax.numpy as jnp
from jax import lax
from jax.experimental import pallas as pl
from jax.experimental.pallas import tpu as pltpu
from jax.sharding import PartitionSpec as P

DH = 128


NEG_FILL = -1e30
LAGS = 3
AXES = ("pb", "z", "core")


def passed_along(block, axis, distance):
    devices = range(lax.axis_size(axis))
    route = [(i - distance, i) for i in devices if i - distance in devices]
    return lax.ppermute(block, axis, route)


def split_parts(value, count):
    parts = []
    for _ in range(count - 1):
        upper = value.astype(jnp.bfloat16).astype(jnp.float32)
        parts.append(upper)
        value = value - upper
    return parts + [value]


def joined(parts, head_count):
    total = parts[..., :head_count]
    for part in range(1, parts.shape[-1] // head_count):
        total = total + parts[..., part * head_count : (part + 1) * head_count]
    return total


def pair_kernel(info_ref, q_ref, k0_ref, k1_ref, v0_ref, v1_ref, out_ref, stat_ref):
    t = pl.program_id(0)
    chip = info_ref[0]
    core = info_ref[1]
    block_len = out_ref.shape[0]
    feature_width = k0_ref.shape[1]
    k_refs = (k0_ref, k1_ref)
    v_refs = (v0_ref, v1_ref)
    head_count = feature_width // DH
    column = 2 * t + core
    q_pos = lax.broadcasted_iota(jnp.int32, (block_len, 2 * block_len), 0)
    k_pos = lax.broadcasted_iota(jnp.int32, (block_len, 2 * block_len), 1)
    first = k_pos < block_len
    starts = []
    masks = []
    stat_ref[...] = jnp.zeros_like(stat_ref)
    for j in range(2):
        key_class = 2 * chip + (core + j) % 2
        lag_a = jnp.where(key_class <= column, 0, 1)
        base = 2 + (t * 2 + j) * LAGS + lag_a
        listed_a = info_ref[base] != 0
        listed_b = info_ref[base + 1] != 0
        diagonal = key_class == column
        reach_a = jnp.where(listed_a, jnp.where(diagonal, 0, block_len), -4 * block_len)
        reach_b = jnp.where(listed_b, block_len, -4 * block_len)
        limit = jnp.where(first, q_pos + reach_a, q_pos + (block_len + reach_b))
        masks.append(k_pos <= limit)
        starts.append(pl.multiple_of(lag_a * block_len, block_len))
    scaling = 1.0 / math.sqrt(DH)
    nt = (((1,), (1,)), ((), ()))
    for h in range(head_count):
        cols = slice(h * DH, (h + 1) * DH)
        q = q_ref[:, cols]
        scores = []
        for j in range(2):
            keys = k_refs[j][pl.ds(starts[j], 2 * block_len), cols]
            s = lax.dot_general(q, keys, nt, preferred_element_type=jnp.float32)
            scores.append(jnp.where(masks[j], s * scaling, NEG_FILL))
        highest = jnp.maximum(
            jnp.max(scores[0], axis=1, keepdims=True), jnp.max(scores[1], axis=1, keepdims=True)
        )
        total = None
        blended = None
        for j in range(2):
            w = jnp.where(masks[j], jnp.exp(scores[j] - highest), 0.0)
            part_total = jnp.sum(w, axis=1, keepdims=True)
            part = jnp.dot(
                w.astype(jnp.bfloat16),
                v_refs[j][pl.ds(starts[j], 2 * block_len), cols],
                preferred_element_type=jnp.float32,
            )
            total = part_total if total is None else total + part_total
            blended = part if blended is None else blended + part
        out_ref[:, cols] = blended.astype(jnp.bfloat16)
        for part, value in enumerate(split_parts(highest, 3) + split_parts(total, 2)):
            stat_ref[:, part * head_count + h : part * head_count + h + 1] = value
    out_ref[:, feature_width:] = stat_ref[...].astype(jnp.bfloat16)


def pair_partials(info, row_q, key_window, value_window):
    block_len = key_window[0].shape[0] // LAGS
    sources = row_q.shape[0] // block_len
    feature_width = key_window[0].shape[1]
    head_count = feature_width // DH
    grid_spec = pltpu.PrefetchScalarGridSpec(
        num_scalar_prefetch=1,
        grid=(sources,),
        in_specs=[
            pl.BlockSpec((block_len, row_q.shape[1]), lambda t, info_ref: (t, 0)),
            pl.BlockSpec(key_window[0].shape, lambda t, info_ref: (0, 0)),
            pl.BlockSpec(key_window[0].shape, lambda t, info_ref: (0, 0)),
            pl.BlockSpec(key_window[0].shape, lambda t, info_ref: (0, 0)),
            pl.BlockSpec(key_window[0].shape, lambda t, info_ref: (0, 0)),
        ],
        out_specs=pl.BlockSpec((block_len, row_q.shape[1]), lambda t, info_ref: (t, 0)),
        scratch_shapes=[pltpu.VMEM((block_len, row_q.shape[1] - feature_width), jnp.float32)],
    )
    return pl.pallas_call(
        pair_kernel,
        grid_spec=grid_spec,
        out_shape=jax.ShapeDtypeStruct(row_q.shape, jnp.bfloat16),
        cost_estimate=pl.CostEstimate(
            flops=sources * head_count * 2 * 2 * 2 * block_len * 2 * block_len * DH,
            transcendentals=sources * head_count * 2 * 2 * block_len * block_len,
            bytes_accessed=2 * sources * block_len * row_q.shape[1] * 2
            + 2 * 2 * LAGS * block_len * feature_width * 2,
        ),
    )(info, row_q, *key_window, *value_window)


def per_device(queries, keys, values, adjacency, counts):
    block_len, feature_width = queries.shape
    head_count = feature_width // DH
    rows = lax.axis_size("pb")
    chips = lax.axis_size("z")
    cores = lax.axis_size("core")
    stripe_count = chips * cores
    chip = lax.axis_index("z")
    core = lax.axis_index("core")
    row_index = lax.axis_index("pb")

    stacked = jnp.stack([keys, values])

    swap = [(0, 1), (1, 0)]
    lag_1 = passed_along(stacked, "pb", 1)
    lag_2 = passed_along(lag_1, "pb", 1)
    own = [stacked, lag_1, lag_2]
    partner = [lax.ppermute(x, "core", swap) for x in own]
    key_window = [jnp.concatenate([x[0] for x in side]) for side in (own, partner)]
    value_window = [jnp.concatenate([x[1] for x in side]) for side in (own, partner)]

    lag_ids = jnp.arange(LAGS, dtype=jnp.int32)
    class_ids = jnp.arange(stripe_count, dtype=jnp.int32)
    slot_ids = jnp.arange(adjacency.shape[1], dtype=jnp.int32)
    wanted = (row_index - lag_ids[None, :]) * stripe_count + class_ids[:, None]
    listed = (adjacency[0][None, None, :] == wanted[:, :, None]) & (
        slot_ids[None, None, :] < counts[0]
    )
    marks = jnp.any(listed, axis=2).reshape(1, -1).astype(jnp.bfloat16)
    spare = jnp.zeros((block_len, DH), jnp.bfloat16)
    spare = lax.dynamic_update_slice(spare, marks, (0, 0))
    row_q = lax.all_gather(
        jnp.concatenate([queries, spare], axis=1), "z", axis=0, tiled=True
    )
    marks_all = row_q.reshape(chips, block_len, -1)[:, 0, feature_width : feature_width + stripe_count * LAGS]
    marks_all = marks_all.reshape(chips, stripe_count, LAGS).astype(jnp.int32)
    mine = [
        lax.dynamic_index_in_dim(marks_all, 2 * chip + (core + j) % 2, axis=1, keepdims=False)
        for j in range(2)
    ]
    info = jnp.concatenate(
        [jnp.stack([chip, core]).astype(jnp.int32), jnp.stack(mine, axis=1).reshape(-1)]
    )

    pair_out = pair_partials(info, row_q, key_window, value_window)
    pair_out = pair_out.reshape(chips, block_len, -1)

    def decode(block):
        stats = block[:, feature_width : feature_width + 5 * head_count].astype(jnp.float32)
        values = block[:, :feature_width].astype(jnp.float32).reshape(block_len, head_count, DH)
        return values, joined(stats[:, : 3 * head_count], head_count), joined(
            stats[:, 3 * head_count :], head_count
        )

    def merged(blocks):
        decoded = [decode(b) for b in blocks]
        top = decoded[0][1]
        for _, m, _ in decoded[1:]:
            top = jnp.maximum(top, m)
        values = None
        total = None
        for v, m, l in decoded:
            f = jnp.exp(m - top)
            values = f[..., None] * v if values is None else values + f[..., None] * v
            total = f * l if total is None else total + f * l
        return values, top, total

    def encoded(values, top, total):
        parts = split_parts(top, 3) + split_parts(total, 2)
        spare = jnp.zeros((block_len, DH - 5 * head_count), jnp.float32)
        stats = jnp.concatenate(parts + [spare], axis=1)
        return jnp.concatenate(
            [values.reshape(block_len, feature_width), stats], axis=1
        ).astype(jnp.bfloat16)

    def block_for(offset):
        return lax.dynamic_index_in_dim(pair_out, (chip + offset) % chips, axis=0, keepdims=False)

    rightward = [(z, (z + 1) % chips) for z in range(chips)]
    leftward = [(z, (z - 1) % chips) for z in range(chips)]
    reach_r = chips // 2
    reach_l = chips - 1 - reach_r
    acc_r = block_for(reach_r)
    acc_l = block_for(-reach_l)
    for step in range(1, reach_r):
        acc_r = encoded(*merged([lax.ppermute(acc_r, "z", rightward), block_for(reach_r - step)]))
        if step < reach_l:
            acc_l = encoded(
                *merged([lax.ppermute(acc_l, "z", leftward), block_for(step - reach_l)])
            )
    final = [block_for(0), lax.ppermute(acc_r, "z", rightward)]
    if reach_l > 0:
        final.append(lax.ppermute(acc_l, "z", leftward))
    values, top, total = merged(final)
    return (values / total[..., None]).reshape(block_len, feature_width).astype(jnp.bfloat16)


def solution(mesh):
    pb, ka = mesh.devices.shape
    grid = jax.sharding.Mesh(mesh.devices.reshape(pb, ka // 2, 2), AXES)
    rows = P(AXES, None)
    in_specs = (rows, rows, rows, rows, P(AXES))
    return jax.shard_map(
        per_device, mesh=grid, in_specs=in_specs, out_specs=rows, check_vma=False
    )
```

```python
import math

import jax
import jax.numpy as jnp
from jax import lax
from jax.experimental import pallas as pl
from jax.experimental.pallas import tpu as pltpu
from jax.sharding import PartitionSpec as P

DH = 128


NEG_FILL = -1e30
LAGS = 3
AXES = ("pb", "z", "core")


def passed_along(block, axis, distance):
    devices = range(lax.axis_size(axis))
    route = [(i - distance, i) for i in devices if i - distance in devices]
    return lax.ppermute(block, axis, route)


def split_parts(value, count):
    parts = []
    for _ in range(count - 1):
        upper = value.astype(jnp.bfloat16).astype(jnp.float32)
        parts.append(upper)
        value = value - upper
    return parts + [value]


def joined(parts, head_count):
    total = parts[..., :head_count]
    for part in range(1, parts.shape[-1] // head_count):
        total = total + parts[..., part * head_count : (part + 1) * head_count]
    return total


def pair_kernel(info_ref, q_ref, k0_ref, k1_ref, v0_ref, v1_ref, out_ref, stat_ref):
    t = pl.program_id(0)
    chip = info_ref[0]
    core = info_ref[1]
    block_len = out_ref.shape[0]
    feature_width = k0_ref.shape[1]
    k_refs = (k0_ref, k1_ref)
    v_refs = (v0_ref, v1_ref)
    head_count = feature_width // DH
    column = 2 * t + core
    q_pos = lax.broadcasted_iota(jnp.int32, (block_len, 2 * block_len), 0)
    k_pos = lax.broadcasted_iota(jnp.int32, (block_len, 2 * block_len), 1)
    first = k_pos < block_len
    starts = []
    masks = []
    stat_ref[...] = jnp.zeros_like(stat_ref)
    for j in range(2):
        key_class = 2 * chip + (core + j) % 2
        lag_a = jnp.where(key_class <= column, 0, 1)
        base = 2 + (t * 2 + j) * LAGS + lag_a
        listed_a = info_ref[base] != 0
        listed_b = info_ref[base + 1] != 0
        diagonal = key_class == column
        reach_a = jnp.where(listed_a, jnp.where(diagonal, 0, block_len), -4 * block_len)
        reach_b = jnp.where(listed_b, block_len, -4 * block_len)
        limit = jnp.where(first, q_pos + reach_a, q_pos + (block_len + reach_b))
        masks.append(k_pos <= limit)
        starts.append(pl.multiple_of(lag_a * block_len, block_len))
    scaling = 1.0 / math.sqrt(DH)
    nt = (((1,), (1,)), ((), ()))
    for h in range(head_count):
        cols = slice(h * DH, (h + 1) * DH)
        q = q_ref[:, cols]
        scores = []
        for j in range(2):
            keys = k_refs[j][pl.ds(starts[j], 2 * block_len), cols]
            s = lax.dot_general(q, keys, nt, preferred_element_type=jnp.float32)
            scores.append(jnp.where(masks[j], s * scaling, NEG_FILL))
        highest = jnp.maximum(
            jnp.max(scores[0], axis=1, keepdims=True), jnp.max(scores[1], axis=1, keepdims=True)
        )
        total = None
        blended = None
        for j in range(2):
            w = jnp.where(masks[j], jnp.exp(scores[j] - highest), 0.0)
            part_total = jnp.sum(w, axis=1, keepdims=True)
            part = jnp.dot(
                w.astype(jnp.bfloat16),
                v_refs[j][pl.ds(starts[j], 2 * block_len), cols],
                preferred_element_type=jnp.float32,
            )
            total = part_total if total is None else total + part_total
            blended = part if blended is None else blended + part
        out_ref[:, cols] = blended.astype(jnp.bfloat16)
        for part, value in enumerate(split_parts(highest, 3) + split_parts(total, 2)):
            stat_ref[:, part * head_count + h : part * head_count + h + 1] = value
    out_ref[:, feature_width:] = stat_ref[...].astype(jnp.bfloat16)


def pair_partials(info, row_q, key_window, value_window):
    block_len = key_window[0].shape[0] // LAGS
    sources = row_q.shape[0] // block_len
    feature_width = key_window[0].shape[1]
    head_count = feature_width // DH
    grid_spec = pltpu.PrefetchScalarGridSpec(
        num_scalar_prefetch=1,
        grid=(sources,),
        in_specs=[
            pl.BlockSpec((block_len, row_q.shape[1]), lambda t, info_ref: (t, 0)),
            pl.BlockSpec(key_window[0].shape, lambda t, info_ref: (0, 0)),
            pl.BlockSpec(key_window[0].shape, lambda t, info_ref: (0, 0)),
            pl.BlockSpec(key_window[0].shape, lambda t, info_ref: (0, 0)),
            pl.BlockSpec(key_window[0].shape, lambda t, info_ref: (0, 0)),
        ],
        out_specs=pl.BlockSpec((block_len, row_q.shape[1]), lambda t, info_ref: (t, 0)),
        scratch_shapes=[pltpu.VMEM((block_len, row_q.shape[1] - feature_width), jnp.float32)],
    )
    return pl.pallas_call(
        pair_kernel,
        grid_spec=grid_spec,
        out_shape=jax.ShapeDtypeStruct(row_q.shape, jnp.bfloat16),
        cost_estimate=pl.CostEstimate(
            flops=sources * head_count * 2 * 2 * 2 * block_len * 2 * block_len * DH,
            transcendentals=sources * head_count * 2 * 2 * block_len * block_len,
            bytes_accessed=2 * sources * block_len * row_q.shape[1] * 2
            + 2 * 2 * LAGS * block_len * feature_width * 2,
        ),
    )(info, row_q, *key_window, *value_window)


def per_device(queries, keys, values, adjacency, counts):
    block_len, feature_width = queries.shape
    head_count = feature_width // DH
    rows = lax.axis_size("pb")
    chips = lax.axis_size("z")
    cores = lax.axis_size("core")
    stripe_count = chips * cores
    chip = lax.axis_index("z")
    core = lax.axis_index("core")
    row_index = lax.axis_index("pb")

    swap = [(0, 1), (1, 0)]
    windows = []
    for block in (keys, values):
        lag_1 = passed_along(block, "pb", 1)
        lag_2 = passed_along(lag_1, "pb", 1)
        own = [block, lag_1, lag_2]
        partner = [lax.ppermute(x, "core", swap) for x in own]
        windows.append([jnp.concatenate(side) for side in (own, partner)])
    key_window, value_window = windows

    lag_ids = jnp.arange(LAGS, dtype=jnp.int32)
    class_ids = jnp.arange(stripe_count, dtype=jnp.int32)
    slot_ids = jnp.arange(adjacency.shape[1], dtype=jnp.int32)
    wanted = (row_index - lag_ids[None, :]) * stripe_count + class_ids[:, None]
    listed = (adjacency[0][None, None, :] == wanted[:, :, None]) & (
        slot_ids[None, None, :] < counts[0]
    )
    marks = jnp.any(listed, axis=2).reshape(1, -1).astype(jnp.bfloat16)
    spare = jnp.zeros((block_len, DH), jnp.bfloat16)
    spare = lax.dynamic_update_slice(spare, marks, (0, 0))
    row_q = lax.all_gather(
        jnp.concatenate([queries, spare], axis=1), "z", axis=0, tiled=True
    )
    marks_all = row_q.reshape(chips, block_len, -1)[:, 0, feature_width : feature_width + stripe_count * LAGS]
    marks_all = marks_all.reshape(chips, stripe_count, LAGS).astype(jnp.int32)
    mine = [
        lax.dynamic_index_in_dim(marks_all, 2 * chip + (core + j) % 2, axis=1, keepdims=False)
        for j in range(2)
    ]
    info = jnp.concatenate(
        [jnp.stack([chip, core]).astype(jnp.int32), jnp.stack(mine, axis=1).reshape(-1)]
    )

    pair_out = pair_partials(info, row_q, key_window, value_window)
    pair_out = pair_out.reshape(chips, block_len, -1)

    def decode(block):
        stats = block[:, feature_width : feature_width + 5 * head_count].astype(jnp.float32)
        values = block[:, :feature_width].astype(jnp.float32).reshape(block_len, head_count, DH)
        return values, joined(stats[:, : 3 * head_count], head_count), joined(
            stats[:, 3 * head_count :], head_count
        )

    def merged(blocks):
        decoded = [decode(b) for b in blocks]
        top = decoded[0][1]
        for _, m, _ in decoded[1:]:
            top = jnp.maximum(top, m)
        values = None
        total = None
        for v, m, l in decoded:
            f = jnp.exp(m - top)
            values = f[..., None] * v if values is None else values + f[..., None] * v
            total = f * l if total is None else total + f * l
        return values, top, total

    def encoded(values, top, total):
        parts = split_parts(top, 3) + split_parts(total, 2)
        spare = jnp.zeros((block_len, DH - 5 * head_count), jnp.float32)
        stats = jnp.concatenate(parts + [spare], axis=1)
        return jnp.concatenate(
            [values.reshape(block_len, feature_width), stats], axis=1
        ).astype(jnp.bfloat16)

    def block_for(offset):
        return lax.dynamic_index_in_dim(pair_out, (chip + offset) % chips, axis=0, keepdims=False)

    rightward = [(z, (z + 1) % chips) for z in range(chips)]
    leftward = [(z, (z - 1) % chips) for z in range(chips)]
    reach_r = chips // 2
    reach_l = chips - 1 - reach_r
    acc_r = block_for(reach_r)
    acc_l = block_for(-reach_l)
    for step in range(1, reach_r):
        acc_r = encoded(*merged([lax.ppermute(acc_r, "z", rightward), block_for(reach_r - step)]))
        if step < reach_l:
            acc_l = encoded(
                *merged([lax.ppermute(acc_l, "z", leftward), block_for(step - reach_l)])
            )
    final = [block_for(0), lax.ppermute(acc_r, "z", rightward)]
    if reach_l > 0:
        final.append(lax.ppermute(acc_l, "z", leftward))
    values, top, total = merged(final)
    return (values / total[..., None]).reshape(block_len, feature_width).astype(jnp.bfloat16)


def solution(mesh):
    pb, ka = mesh.devices.shape
    grid = jax.sharding.Mesh(mesh.devices.reshape(pb, ka // 2, 2), AXES)
    rows = P(AXES, None)
    in_specs = (rows, rows, rows, rows, P(AXES))
    return jax.shard_map(
        per_device, mesh=grid, in_specs=in_specs, out_specs=rows, check_vma=False
    )
```
